32 devices in a mesh: seq: 8 (over y, x, core), head: 4 (over z).
Axes of the slice: x: 2, y: 2, z: 4, core: 2. Of those that a mesh axis runs over, the one named last changes fastest.
Arguments:
- query_rows: bfloat16 [4096, 8192], P(('seq', 'head')), may hold values from -150 to 150
- key_rows: bfloat16 [4096, 1024], P(('seq', 'head')), may hold values from -5 to 5
- value_rows: bfloat16 [4096, 1024], P(('seq', 'head')), may hold values from -6 to 6
- doc_ids: int32 [4096], replicated, may hold values from 0 to 1, never falling along the last dimension, each value on 1 to 3584 neighbouring positions
Outputs:
- attended: bfloat16 [4096, 8192], P(('seq', 'head'))
The draws below stay inside these ranges and needn't reach their ends.
Inputs may be any that keep to these rules, and one draw needn't show every extreme that they name: `doc_ids`: never falls along the pack; each document has 1 to 3584 tokens.
All inputs are finite; a program needn't handle non-finite values.
Results may differ from the reference program's by a relative error of at most 0.0039.
Values may be sent and summed in bfloat16 or wider, within the bound.
No kernel may reach another device: no remote copies, remote signals or barrier semaphores. Data moves between devices by JAX's collectives and lax.ppermute only.
A program may use at most 128 MiB of HBM per device.

```python
import math
import jax
import jax.numpy as jnp
import numpy as np
from jax import lax

HEADS = 64
KV_HEADS = 8
HEAD_DIM = 128
TOK_DEV = 512
SPAN = 7
TOKENS = 4096
DOC_MOST = 3584
DOC_COUNT = 2


def drawn_pair(key):
    folded = jax.random.fold_in(key, 7)
    key_draw, query_draw = jax.random.split(folded, 2)
    heads_per = HEADS // KV_HEADS
    key_heads = jnp.clip(jax.random.normal(key_draw, (TOKENS, KV_HEADS, HEAD_DIM), jnp.float32), -5.0, 5.0)
    query_heads = jnp.clip(jax.random.normal(query_draw, (TOKENS, KV_HEADS, heads_per, HEAD_DIM), jnp.float32), -5.0, 5.0)
    return (query_heads.reshape(TOKENS, HEADS * HEAD_DIM), key_heads.reshape(TOKENS, KV_HEADS * HEAD_DIM))


def draw_query_rows(key, part):
    return drawn_pair(key)[0].astype(jnp.bfloat16)


def draw_key_rows(key, part):
    return drawn_pair(key)[1].astype(jnp.bfloat16)


def block_levels(stream_key, shape, cuts, least, high):
    gain, own = 1.0, jax.random.fold_in(stream_key, 6)
    for dim, shards_of in cuts:
        heights = jnp.exp(jax.random.uniform(jax.random.fold_in(own, dim), (shards_of,), jnp.float32, least / len(cuts), high / len(cuts)))
        gain = gain * jnp.repeat(heights, shape[dim] // shards_of).reshape([-1 if axis == dim else 1 for axis in range(len(shape))])
    return gain


def length_profile(amount, total, limit, lean):
    loads = [(1 << 20) // math.isqrt(grade ** lean) + 1 for grade in range(2, amount + 1)]
    rest, given = total - limit - (amount - 1), [1] * (amount - 1)
    while rest > 0:
        candidates = [i for i in range(amount - 1) if given[i] < limit]
        pool, remaining = sum([loads[i] for i in candidates]), rest
        for i in candidates:
            more = min(limit - given[i], max(1, remaining * loads[i] // pool), rest)
            given[i] = given[i] + more
            rest = rest - more
    return np.array([limit] + given)


def ragged(rng, number_of, total, most, lean):
    if number_of == 2:
        one = jax.random.randint(rng, (), max(1, total - most), min(most, total - 1) + 1)
        return jnp.stack([one, total - one])
    tallies = jnp.asarray(length_profile(number_of, total, most, lean), jnp.int32)
    twos = (number_of - 1) // 2
    donor, sink = tallies[1:1 + 2 * twos:2], tallies[2:2 + 2 * twos:2]
    room = jnp.minimum(donor - 1, most - sink)
    shifted = jax.random.randint(jax.random.fold_in(rng, 1), (twos,), 0, 1 << 20) % (room + 1)
    tallies = tallies.at[1:1 + 2 * twos:2].set(donor - shifted).at[2:2 + 2 * twos:2].set(sink + shifted)
    return tallies[jax.random.permutation(jax.random.fold_in(rng, 2), number_of)]


def gaussian(key, extent, width, limit, shards=(), held_as=jnp.bfloat16):
    entries = width * jax.random.normal(key, extent, jnp.float32)
    if shards:
        entries = entries * block_levels(key, extent, shards, -0.22, 0.18)
    return jnp.clip(entries, -limit, limit).astype(held_as)


def setup_inputs(seed: int = 0) -> dict:
    arg_keys = jax.random.split(jax.random.key(seed), 5)
    query_rows = draw_query_rows(jax.random.fold_in(arg_keys[4], 71), 0)
    key_rows = draw_key_rows(jax.random.fold_in(arg_keys[4], 71), 0)
    value_rows = gaussian(arg_keys[2], (TOKENS, KV_HEADS * HEAD_DIM), 1.0, 6.0, ((0, 32),))
    doc_ids = jnp.searchsorted(jnp.cumsum(ragged(arg_keys[3], DOC_COUNT, TOKENS, DOC_MOST, 2)), jnp.arange(TOKENS), side="right").astype(jnp.int32)
    return dict(query_rows=query_rows, key_rows=key_rows, value_rows=value_rows, doc_ids=doc_ids)


def reference(query_rows, key_rows, value_rows, doc_ids):
    tokens = query_rows.shape[0]
    block_rows = TOK_DEV
    window = (SPAN + 1) * TOK_DEV
    heads_per = HEADS // KV_HEADS
    score_scale = 1.0 / (HEAD_DIM ** 0.5)
    query_heads = query_rows.reshape(tokens, KV_HEADS, heads_per, HEAD_DIM)
    key_heads = key_rows.reshape(tokens, KV_HEADS, HEAD_DIM)
    value_heads = value_rows.reshape(tokens, KV_HEADS, HEAD_DIM)

    def attend_rows(block_index):
        query_start = (block_index * block_rows).astype(jnp.int32)
        key_start = jnp.clip(query_start - SPAN * block_rows, 0, tokens - window).astype(jnp.int32)
        query_block = lax.dynamic_slice_in_dim(query_heads, query_start, block_rows, 0)
        key_block = lax.dynamic_slice_in_dim(key_heads, key_start, window, 0)
        value_block = lax.dynamic_slice_in_dim(value_heads, key_start, window, 0)
        query_pos = query_start + jnp.arange(block_rows, dtype=jnp.int32)
        key_pos = key_start + jnp.arange(window, dtype=jnp.int32)
        query_doc = lax.dynamic_slice_in_dim(doc_ids, query_start, block_rows, 0)
        key_doc = lax.dynamic_slice_in_dim(doc_ids, key_start, window, 0)
        visible = (key_pos[None, :] <= query_pos[:, None]) & (key_doc[None, :] == query_doc[:, None])

        def attend_group(group_index):
            query_group = lax.dynamic_index_in_dim(query_block, group_index, 1, keepdims=False)
            key_group = lax.dynamic_index_in_dim(key_block, group_index, 1, keepdims=False)
            value_group = lax.dynamic_index_in_dim(value_block, group_index, 1, keepdims=False)
            scores = jnp.einsum('qrd,kd->rqk', query_group.astype(jnp.float32), key_group.astype(jnp.float32)) * score_scale
            scores = jnp.where(visible[None, :, :], scores, -jnp.inf)
            row_max = jnp.max(scores, axis=-1, keepdims=True)
            weights = jnp.exp(scores - row_max)
            denominator = jnp.sum(weights, axis=-1)
            rounded = lax.optimization_barrier(weights.astype(jnp.bfloat16))
            mixed = jnp.einsum('rqk,kd->qrd', rounded.astype(jnp.float32), value_group.astype(jnp.float32))
            mixed = mixed / jnp.transpose(denominator)[:, :, None]
            return mixed.astype(jnp.bfloat16)

        grouped = lax.map(attend_group, jnp.arange(KV_HEADS, dtype=jnp.int32))
        return jnp.transpose(grouped, (1, 0, 2, 3)).reshape(block_rows, HEADS * HEAD_DIM)

    blocks_out = lax.map(attend_rows, jnp.arange(tokens // block_rows, dtype=jnp.int32))
    return blocks_out.reshape(tokens, HEADS * HEAD_DIM)
```

```python
import functools

import jax
import jax.numpy as jnp
from jax import lax
from jax.experimental import pallas as pl
from jax.experimental.pallas import tpu as pltpu
from jax.sharding import PartitionSpec as P

HEAD_DIM = 128
DOC_MOST = 3584
NEG_START = -1e30


def flash_kernel(meta_ref, q_ref, k_ref, v_ref, qdoc_ref, kdoc_ref, o_ref, m_sc, l_sc, acc_sc,
                 *, heads_per, rows, steps, scale):
    step = pl.program_id(1)
    first_block = meta_ref[0]
    own_block = meta_ref[1]
    key_block = first_block + step

    @pl.when(step == 0)
    def _():
        m_sc[...] = jnp.full(m_sc.shape, NEG_START, jnp.float32)
        l_sc[...] = jnp.zeros(l_sc.shape, jnp.float32)
        acc_sc[...] = jnp.zeros(acc_sc.shape, jnp.float32)

    @pl.when(key_block <= own_block)
    def _():
        query_pos = own_block * rows + lax.broadcasted_iota(jnp.int32, (rows, rows), 0)
        key_pos = key_block * rows + lax.broadcasted_iota(jnp.int32, (rows, rows), 1)
        visible = (key_pos <= query_pos) & (kdoc_ref[...] == qdoc_ref[...])
        keys = k_ref[...]
        values = v_ref[...]
        for r in range(heads_per):
            cols = slice(r * HEAD_DIM, (r + 1) * HEAD_DIM)
            scores = lax.dot_general(
                q_ref[:, cols], keys, (((1,), (1,)), ((), ())), preferred_element_type=jnp.float32
            ) * scale
            scores = jnp.where(visible, scores, -jnp.inf)
            m_old = m_sc[r]
            m_new = jnp.maximum(m_old, jnp.max(scores, axis=-1, keepdims=True))
            weights = jnp.exp(scores - m_new)
            factor = jnp.exp(m_old - m_new)
            l_sc[r] = l_sc[r] * factor + jnp.sum(weights, axis=-1, keepdims=True)
            product = jnp.dot(weights.astype(jnp.bfloat16), values, preferred_element_type=jnp.float32)
            acc_sc[:, cols] = acc_sc[:, cols] * factor + product
            m_sc[r] = m_new

    @pl.when(step == steps - 1)
    def _():
        for r in range(heads_per):
            cols = slice(r * HEAD_DIM, (r + 1) * HEAD_DIM)
            o_ref[:, cols] = (acc_sc[:, cols] / l_sc[r]).astype(o_ref.dtype)


def attend(meta, q_local, key_piece, value_piece, doc_ids, groups, heads_per, rows):
    tokens = doc_ids.shape[0]
    blocks = tokens // rows
    steps = min(blocks, -(-DOC_MOST // rows) + 1)
    width = heads_per * HEAD_DIM

    def kv_map(g, j, meta):
        return (jnp.minimum(meta[0] + j, meta[1]), g)

    kernel = functools.partial(
        flash_kernel, heads_per=heads_per, rows=rows, steps=steps, scale=1.0 / HEAD_DIM**0.5
    )
    return pl.pallas_call(
        kernel,
        out_shape=jax.ShapeDtypeStruct((rows, groups * width), jnp.bfloat16),
        grid_spec=pltpu.PrefetchScalarGridSpec(
            num_scalar_prefetch=1,
            grid=(groups, steps),
            in_specs=[
                pl.BlockSpec((rows, width), lambda g, j, meta: (0, g)),
                pl.BlockSpec((rows, HEAD_DIM), kv_map),
                pl.BlockSpec((rows, HEAD_DIM), kv_map),
                pl.BlockSpec((rows, 1), lambda g, j, meta: (meta[1], 0)),
                pl.BlockSpec((1, rows), lambda g, j, meta: (0, jnp.minimum(meta[0] + j, meta[1]))),
            ],
            out_specs=pl.BlockSpec((rows, width), lambda g, j, meta: (0, g)),
            scratch_shapes=[
                pltpu.VMEM((heads_per, rows, 1), jnp.float32),
                pltpu.VMEM((heads_per, rows, 1), jnp.float32),
                pltpu.VMEM((rows, width), jnp.float32),
            ],
        ),
        compiler_params=pltpu.CompilerParams(dimension_semantics=("arbitrary", "arbitrary")),
    )(meta, q_local, key_piece, value_piece, doc_ids.reshape(tokens, 1), doc_ids.reshape(1, tokens))


def body(query_rows, key_rows, value_rows, doc_ids):
    q_local, key_local, value_local = (
        lax.all_to_all(query_rows, "head", split_axis=1, concat_axis=0, tiled=True),
        lax.all_to_all(key_rows, "head", split_axis=1, concat_axis=0, tiled=True),
        lax.all_to_all(value_rows, "head", split_axis=1, concat_axis=0, tiled=True),
    )
    rows = q_local.shape[0]
    groups = key_local.shape[1] // HEAD_DIM
    heads_per = q_local.shape[1] // key_local.shape[1]
    own_block = lax.axis_index("seq")
    first_doc = doc_ids[own_block * rows]
    doc_start = jnp.sum((doc_ids < first_doc).astype(jnp.int32))
    meta = jnp.stack([doc_start // rows, own_block]).astype(jnp.int32)
    key_piece = lax.all_gather(key_local, "seq", axis=0, tiled=True)
    value_piece = lax.all_gather(value_local, "seq", axis=0, tiled=True)
    result = attend(meta, q_local, key_piece, value_piece, doc_ids, groups, heads_per, rows)
    return lax.all_to_all(result, "head", split_axis=0, concat_axis=1, tiled=True)


def solution(mesh):
    placed = (P(("seq", "head"), None), P(("seq", "head"), None), P(("seq", "head"), None), P())
    return jax.shard_map(
        body, mesh=mesh, in_specs=placed, out_specs=P(("seq", "head"), None), check_vma=False
    )
```

```python
import functools

import jax
import jax.numpy as jnp
from jax import lax
from jax.experimental import pallas as pl
from jax.experimental.pallas import tpu as pltpu
from jax.sharding import PartitionSpec as P

HEAD_DIM = 128
KEY_ROWS = 512
DOC_MOST = 3584
NEG_START = -1e30


def flash_kernel(meta_ref, doc_ref, q_ref, k_ref, v_ref, qdoc_ref, kdoc_ref, o_ref, m_sc, l_sc, acc_sc,
                 *, heads_per, groups, q_rows, steps, scale):
    step = pl.program_id(0)
    first_block = meta_ref[0]
    last_block = meta_ref[1]
    q_off = meta_ref[2]
    key_block = jnp.minimum(first_block + step, last_block)
    active = first_block + step <= last_block
    full = (key_block * KEY_ROWS + KEY_ROWS - 1 < q_off) & (
        doc_ref[key_block * KEY_ROWS] == doc_ref[q_off + q_rows - 1]
    )

    @pl.when(step == 0)
    def _():
        m_sc[...] = jnp.full(m_sc.shape, NEG_START, jnp.float32)
        l_sc[...] = jnp.zeros(l_sc.shape, jnp.float32)
        acc_sc[...] = jnp.zeros(acc_sc.shape, jnp.float32)

    def compute(masked):
        if masked:
            query_pos = q_off + lax.broadcasted_iota(jnp.int32, (q_rows, KEY_ROWS), 0)
            key_pos = key_block * KEY_ROWS + lax.broadcasted_iota(jnp.int32, (q_rows, KEY_ROWS), 1)
            visible = (key_pos <= query_pos) & (kdoc_ref[...] == qdoc_ref[...])
        for g in range(groups):
            keys = k_ref[:, g * HEAD_DIM:(g + 1) * HEAD_DIM]
            values = v_ref[:, g * HEAD_DIM:(g + 1) * HEAD_DIM]
            for r in range(heads_per):
                j = g * heads_per + r
                cols = slice(j * HEAD_DIM, (j + 1) * HEAD_DIM)
                scores = lax.dot_general(
                    q_ref[:, cols], keys, (((1,), (1,)), ((), ())), preferred_element_type=jnp.float32
                ) * scale
                if masked:
                    scores = jnp.where(visible, scores, -jnp.inf)
                m_old = m_sc[j]
                m_new = jnp.maximum(m_old, jnp.max(scores, axis=-1, keepdims=True))
                weights = jnp.exp(scores - m_new)
                factor = jnp.exp(m_old - m_new)
                l_sc[j] = l_sc[j] * factor + jnp.sum(weights, axis=-1, keepdims=True)
                product = jnp.dot(weights.astype(jnp.bfloat16), values, preferred_element_type=jnp.float32)
                acc_sc[:, cols] = acc_sc[:, cols] * factor + product
                m_sc[j] = m_new

    @pl.when(active & full)
    def _():
        compute(False)

    @pl.when(active & jnp.logical_not(full))
    def _():
        compute(True)

    @pl.when(step == steps - 1)
    def _():
        for j in range(groups * heads_per):
            cols = slice(j * HEAD_DIM, (j + 1) * HEAD_DIM)
            o_ref[:, cols] = (acc_sc[:, cols] / l_sc[j]).astype(o_ref.dtype)


def attend(q_tile, q_off, kv_piece, doc_ids, groups, heads_per):
    tokens = doc_ids.shape[0]
    q_rows = q_tile.shape[0]
    blocks = tokens // KEY_ROWS
    steps = min(blocks, -(-DOC_MOST // KEY_ROWS) + 1)
    doc_start = jnp.sum((doc_ids < doc_ids[q_off]).astype(jnp.int32))
    meta = jnp.stack([doc_start // KEY_ROWS, (q_off + q_rows - 1) // KEY_ROWS, q_off]).astype(jnp.int32)
    width = groups * heads_per * HEAD_DIM
    kv_width = groups * HEAD_DIM

    def key_index(j, meta, docs):
        return jnp.minimum(meta[0] + j, meta[1])

    kernel = functools.partial(
        flash_kernel, heads_per=heads_per, groups=groups, q_rows=q_rows, steps=steps,
        scale=1.0 / HEAD_DIM**0.5,
    )
    return pl.pallas_call(
        kernel,
        out_shape=jax.ShapeDtypeStruct((q_rows, width), jnp.bfloat16),
        grid_spec=pltpu.PrefetchScalarGridSpec(
            num_scalar_prefetch=2,
            grid=(steps,),
            in_specs=[
                pl.BlockSpec((q_rows, width), lambda j, meta, docs: (0, 0)),
                pl.BlockSpec((KEY_ROWS, kv_width), lambda j, meta, docs: (key_index(j, meta, docs), 0)),
                pl.BlockSpec((KEY_ROWS, kv_width), lambda j, meta, docs: (key_index(j, meta, docs), 1)),
                pl.BlockSpec((q_rows, 1), lambda j, meta, docs: (meta[2] // q_rows, 0)),
                pl.BlockSpec((1, KEY_ROWS), lambda j, meta, docs: (0, key_index(j, meta, docs))),
            ],
            out_specs=pl.BlockSpec((q_rows, width), lambda j, meta, docs: (0, 0)),
            scratch_shapes=[
                pltpu.VMEM((groups * heads_per, q_rows, 1), jnp.float32),
                pltpu.VMEM((groups * heads_per, q_rows, 1), jnp.float32),
                pltpu.VMEM((q_rows, width), jnp.float32),
            ],
        ),
        compiler_params=pltpu.CompilerParams(dimension_semantics=("arbitrary",)),
    )(meta, doc_ids, q_tile, kv_piece, kv_piece, doc_ids.reshape(tokens, 1), doc_ids.reshape(1, tokens))


def gather_kv(key_rows, value_rows):
    stacked = jnp.stack([key_rows, value_rows], axis=1)
    local = lax.all_to_all(stacked, "head", split_axis=2, concat_axis=0, tiled=True)
    local = local.reshape(local.shape[0], -1)
    return lax.all_gather(local, "seq", axis=0, tiled=True)


def body(query_rows, key_rows, value_rows, doc_ids):
    q_local = lax.all_to_all(query_rows, "head", split_axis=1, concat_axis=0, tiled=True)
    groups = key_rows.shape[1] // HEAD_DIM // lax.axis_size("head")
    heads_per = query_rows.shape[1] // key_rows.shape[1]
    kv_piece = gather_kv(key_rows, value_rows)
    q_off = lax.axis_index("seq") * q_local.shape[0]
    result = attend(q_local, q_off, kv_piece, doc_ids, groups, heads_per)
    return lax.all_to_all(result, "head", split_axis=0, concat_axis=1, tiled=True)


def solution(mesh):
    placed = (P(("seq", "head"), None), P(("seq", "head"), None), P(("seq", "head"), None), P())
    return jax.shard_map(
        body, mesh=mesh, in_specs=placed, out_specs=P(("seq", "head"), None), check_vma=False
    )
```

```python
import functools

import jax
import jax.numpy as jnp
from jax import lax
from jax.experimental import pallas as pl
from jax.experimental.pallas import tpu as pltpu
from jax.sharding import PartitionSpec as P

HEAD_DIM = 128
KEY_ROWS = 512
DOC_MOST = 3584
NEG_START = -1e30


def flash_kernel(meta_ref, doc_ref, q_ref, k_ref, v_ref, qdoc_ref, kdoc_ref, o_ref, m_sc, l_sc, acc_sc,
                 *, heads_per, groups, q_rows, steps, scale):
    step = pl.program_id(0)
    first_block = meta_ref[0]
    last_block = meta_ref[1]
    q_off = meta_ref[2]
    key_block = jnp.minimum(first_block + step, last_block)
    active = first_block + step <= last_block
    full = (key_block * KEY_ROWS + KEY_ROWS - 1 < q_off) & (
        doc_ref[key_block * KEY_ROWS] == doc_ref[q_off + q_rows - 1]
    )

    @pl.when(step == 0)
    def _():
        m_sc[...] = jnp.full(m_sc.shape, NEG_START, jnp.float32)
        l_sc[...] = jnp.zeros(l_sc.shape, jnp.float32)
        acc_sc[...] = jnp.zeros(acc_sc.shape, jnp.float32)

    def compute(masked):
        if masked:
            query_pos = q_off + lax.broadcasted_iota(jnp.int32, (q_rows, KEY_ROWS), 0)
            key_pos = key_block * KEY_ROWS + lax.broadcasted_iota(jnp.int32, (q_rows, KEY_ROWS), 1)
            visible = (key_pos <= query_pos) & (kdoc_ref[...] == qdoc_ref[...])
        for g in range(groups):
            keys = k_ref[:, g * HEAD_DIM:(g + 1) * HEAD_DIM]
            values = v_ref[:, g * HEAD_DIM:(g + 1) * HEAD_DIM]
            for r in range(heads_per):
                j = g * heads_per + r
                cols = slice(j * HEAD_DIM, (j + 1) * HEAD_DIM)
                scores = lax.dot_general(
                    q_ref[:, cols], keys, (((1,), (1,)), ((), ())), preferred_element_type=jnp.float32
                ) * scale
                if masked:
                    scores = jnp.where(visible, scores, -jnp.inf)
                m_old = m_sc[j]
                m_new = jnp.maximum(m_old, jnp.max(scores, axis=-1, keepdims=True))
                weights = jnp.exp(scores - m_new)
                factor = jnp.exp(m_old - m_new)
                l_sc[j] = l_sc[j] * factor + jnp.sum(weights, axis=-1, keepdims=True)
                product = jnp.dot(weights.astype(jnp.bfloat16), values, preferred_element_type=jnp.float32)
                acc_sc[:, cols] = acc_sc[:, cols] * factor + product
                m_sc[j] = m_new

    @pl.when(active & full)
    def _():
        compute(False)

    @pl.when(active & jnp.logical_not(full))
    def _():
        compute(True)

    @pl.when(step == steps - 1)
    def _():
        for j in range(groups * heads_per):
            cols = slice(j * HEAD_DIM, (j + 1) * HEAD_DIM)
            o_ref[:, cols] = (acc_sc[:, cols] / l_sc[j]).astype(o_ref.dtype)


def attend(q_tile, q_off, kv_piece, doc_ids, groups, heads_per):
    tokens = doc_ids.shape[0]
    q_rows = q_tile.shape[0]
    blocks = tokens // KEY_ROWS
    steps = min(blocks, -(-DOC_MOST // KEY_ROWS) + 1)
    doc_start = jnp.sum((doc_ids < doc_ids[q_off]).astype(jnp.int32))
    meta = jnp.stack([doc_start // KEY_ROWS, (q_off + q_rows - 1) // KEY_ROWS, q_off]).astype(jnp.int32)
    width = groups * heads_per * HEAD_DIM
    kv_width = groups * HEAD_DIM

    def key_index(j, meta, docs):
        return jnp.minimum(meta[0] + j, meta[1])

    kernel = functools.partial(
        flash_kernel, heads_per=heads_per, groups=groups, q_rows=q_rows, steps=steps,
        scale=1.0 / HEAD_DIM**0.5,
    )
    return pl.pallas_call(
        kernel,
        out_shape=jax.ShapeDtypeStruct((q_rows, width), jnp.bfloat16),
        grid_spec=pltpu.PrefetchScalarGridSpec(
            num_scalar_prefetch=2,
            grid=(steps,),
            in_specs=[
                pl.BlockSpec((q_rows, width), lambda j, meta, docs: (0, 0)),
                pl.BlockSpec((KEY_ROWS, kv_width), lambda j, meta, docs: (key_index(j, meta, docs), 0)),
                pl.BlockSpec((KEY_ROWS, kv_width), lambda j, meta, docs: (key_index(j, meta, docs), 1)),
                pl.BlockSpec((q_rows, 1), lambda j, meta, docs: (meta[2] // q_rows, 0)),
                pl.BlockSpec((1, KEY_ROWS), lambda j, meta, docs: (0, key_index(j, meta, docs))),
            ],
            out_specs=pl.BlockSpec((q_rows, width), lambda j, meta, docs: (0, 0)),
            scratch_shapes=[
                pltpu.VMEM((groups * heads_per, q_rows, 1), jnp.float32),
                pltpu.VMEM((groups * heads_per, q_rows, 1), jnp.float32),
                pltpu.VMEM((q_rows, width), jnp.float32),
            ],
        ),
        compiler_params=pltpu.CompilerParams(dimension_semantics=("arbitrary",)),
    )(meta, doc_ids, q_tile, kv_piece, kv_piece, doc_ids.reshape(tokens, 1), doc_ids.reshape(1, tokens))


def gather_kv(key_rows, value_rows):
    stacked = jnp.stack([key_rows, value_rows], axis=1)
    local = lax.all_to_all(stacked, "head", split_axis=2, concat_axis=0, tiled=True)
    local = local.reshape(local.shape[0], -1)
    return lax.all_gather(local, "seq", axis=0, tiled=True)


def body(query_rows, key_rows, value_rows, doc_ids):
    head_count = lax.axis_size("head")
    head = lax.axis_index("head")
    sub = query_rows.shape[0]
    q_width = query_rows.shape[1] // head_count
    groups = key_rows.shape[1] // HEAD_DIM // head_count
    heads_per = query_rows.shape[1] // key_rows.shape[1]
    block_start = lax.axis_index("seq") * sub * head_count
    kv_piece = gather_kv(key_rows, value_rows)
    result = jnp.zeros_like(query_rows)
    for t in range(head_count):
        piece = lax.dynamic_slice_in_dim(query_rows, ((head + t) % head_count) * q_width, q_width, axis=1)
        if t:
            piece = lax.ppermute(piece, "head", [(i, (i + t) % head_count) for i in range(head_count)])
        q_off = block_start + ((head - t) % head_count) * sub
        out_tile = attend(piece, q_off, kv_piece, doc_ids, groups, heads_per)
        if t:
            out_tile = lax.ppermute(out_tile, "head", [(i, (i - t) % head_count) for i in range(head_count)])
        result = lax.dynamic_update_slice_in_dim(result, out_tile, ((head + t) % head_count) * q_width, axis=1)
    return result


def solution(mesh):
    placed = (P(("seq", "head"), None), P(("seq", "head"), None), P(("seq", "head"), None), P())
    return jax.shard_map(
        body, mesh=mesh, in_specs=placed, out_specs=P(("seq", "head"), None), check_vma=False
    )
```

```python
import functools
import math

import jax
import jax.numpy as jnp
from jax import lax
from jax.experimental import pallas as pl
from jax.experimental.pallas import tpu as pltpu
from jax.sharding import PartitionSpec as P

HEAD_DIM = 128
KEY_ROWS = 512
DOC_MOST = 3584
NEG_START = -1e30


def flash_kernel(meta_ref, doc_ref, q_ref, kt_ref, v_ref, qdoc_ref, kdoc_ref, o_ref, m_sc, l_sc, acc_sc,
                 *, heads_per, groups, q_rows, steps, scale):
    step = pl.program_id(0)
    first_block = meta_ref[0]
    last_block = meta_ref[1]
    q_off = meta_ref[2]
    key_block = jnp.minimum(first_block + step, last_block)
    active = first_block + step <= last_block
    full = (key_block * KEY_ROWS + KEY_ROWS - 1 < q_off) & (
        doc_ref[key_block * KEY_ROWS] == doc_ref[q_off + q_rows - 1]
    )

    @pl.when(step == 0)
    def _():
        m_sc[...] = jnp.full(m_sc.shape, NEG_START, jnp.float32)
        l_sc[...] = jnp.zeros(l_sc.shape, jnp.float32)
        acc_sc[...] = jnp.zeros(acc_sc.shape, jnp.float32)

    def compute(masked):
        if masked:
            query_pos = q_off + lax.broadcasted_iota(jnp.int32, (q_rows, KEY_ROWS), 0)
            key_pos = key_block * KEY_ROWS + lax.broadcasted_iota(jnp.int32, (q_rows, KEY_ROWS), 1)
            visible = (key_pos <= query_pos) & (kdoc_ref[...] == qdoc_ref[...])
        for g in range(groups):
            keys_t = kt_ref[g * HEAD_DIM:(g + 1) * HEAD_DIM, :]
            values = v_ref[:, g * HEAD_DIM:(g + 1) * HEAD_DIM]
            for r in range(heads_per):
                j = g * heads_per + r
                cols = slice(j * HEAD_DIM, (j + 1) * HEAD_DIM)
                scores = jnp.dot(q_ref[:, cols], keys_t, preferred_element_type=jnp.float32)
                if masked:
                    scores = jnp.where(visible, scores, -jnp.inf)
                m_old = m_sc[j]
                m_new = jnp.maximum(m_old, jnp.max(scores, axis=-1, keepdims=True))
                weights = jnp.exp2((scores - m_new) * scale)
                factor = jnp.exp2((m_old - m_new) * scale)
                l_sc[j] = l_sc[j] * factor + jnp.sum(weights, axis=-1, keepdims=True)
                product = jnp.dot(weights.astype(jnp.bfloat16), values, preferred_element_type=jnp.float32)
                acc_sc[:, cols] = acc_sc[:, cols] * factor + product
                m_sc[j] = m_new

    @pl.when(active & full)
    def _():
        compute(False)

    @pl.when(active & jnp.logical_not(full))
    def _():
        compute(True)

    @pl.when(step == steps - 1)
    def _():
        for j in range(groups * heads_per):
            cols = slice(j * HEAD_DIM, (j + 1) * HEAD_DIM)
            o_ref[:, cols] = (acc_sc[:, cols] / l_sc[j]).astype(o_ref.dtype)


def attend(q_tile, q_off, keys_t, values, doc_ids, groups, heads_per):
    tokens = doc_ids.shape[0]
    q_rows = q_tile.shape[0]
    blocks = tokens // KEY_ROWS
    steps = min(blocks, -(-DOC_MOST // KEY_ROWS) + 1)
    doc_start = jnp.sum((doc_ids < doc_ids[q_off]).astype(jnp.int32))
    meta = jnp.stack([doc_start // KEY_ROWS, (q_off + q_rows - 1) // KEY_ROWS, q_off]).astype(jnp.int32)
    width = groups * heads_per * HEAD_DIM
    kv_width = groups * HEAD_DIM

    def key_index(j, meta, docs):
        return jnp.minimum(meta[0] + j, meta[1])

    kernel = functools.partial(
        flash_kernel, heads_per=heads_per, groups=groups, q_rows=q_rows, steps=steps,
        scale=math.log2(math.e) / HEAD_DIM**0.5,
    )
    return pl.pallas_call(
        kernel,
        out_shape=jax.ShapeDtypeStruct((q_rows, width), jnp.bfloat16),
        grid_spec=pltpu.PrefetchScalarGridSpec(
            num_scalar_prefetch=2,
            grid=(steps,),
            in_specs=[
                pl.BlockSpec((q_rows, width), lambda j, meta, docs: (0, 0)),
                pl.BlockSpec((kv_width, KEY_ROWS), lambda j, meta, docs: (0, key_index(j, meta, docs))),
                pl.BlockSpec((KEY_ROWS, kv_width), lambda j, meta, docs: (key_index(j, meta, docs), 0)),
                pl.BlockSpec((q_rows, 1), lambda j, meta, docs: (meta[2] // q_rows, 0)),
                pl.BlockSpec((1, KEY_ROWS), lambda j, meta, docs: (0, key_index(j, meta, docs))),
            ],
            out_specs=pl.BlockSpec((q_rows, width), lambda j, meta, docs: (0, 0)),
            scratch_shapes=[
                pltpu.VMEM((groups * heads_per, q_rows, 1), jnp.float32),
                pltpu.VMEM((groups * heads_per, q_rows, 1), jnp.float32),
                pltpu.VMEM((q_rows, width), jnp.float32),
            ],
        ),
        compiler_params=pltpu.CompilerParams(dimension_semantics=("arbitrary",)),
    )(meta, doc_ids, q_tile, keys_t, values, doc_ids.reshape(tokens, 1), doc_ids.reshape(1, tokens))


def gather_kv(key_rows, value_rows):
    stacked = jnp.stack([key_rows, value_rows], axis=1)
    local = lax.all_to_all(stacked, "head", split_axis=2, concat_axis=0, tiled=True)
    keys_t = lax.all_gather(local[:, 0, :].T, "seq", axis=1, tiled=True)
    values = lax.all_gather(local[:, 1, :], "seq", axis=0, tiled=True)
    return keys_t, values


def body(query_rows, key_rows, value_rows, doc_ids):
    head_count = lax.axis_size("head")
    head = lax.axis_index("head")
    sub = query_rows.shape[0]
    q_width = query_rows.shape[1] // head_count
    groups = key_rows.shape[1] // HEAD_DIM // head_count
    heads_per = query_rows.shape[1] // key_rows.shape[1]
    block_start = lax.axis_index("seq") * sub * head_count
    keys_t, values = gather_kv(key_rows, value_rows)
    result = jnp.zeros_like(query_rows)
    for t in range(head_count):
        piece = lax.dynamic_slice_in_dim(query_rows, ((head + t) % head_count) * q_width, q_width, axis=1)
        if t:
            piece = lax.ppermute(piece, "head", [(i, (i + t) % head_count) for i in range(head_count)])
        q_off = block_start + ((head - t) % head_count) * sub
        out_tile = attend(piece, q_off, keys_t, values, doc_ids, groups, heads_per)
        if t:
            out_tile = lax.ppermute(out_tile, "head", [(i, (i - t) % head_count) for i in range(head_count)])
        result = lax.dynamic_update_slice_in_dim(result, out_tile, ((head + t) % head_count) * q_width, axis=1)
    return result


def solution(mesh):
    placed = (P(("seq", "head"), None), P(("seq", "head"), None), P(("seq", "head"), None), P())
    return jax.shard_map(
        body, mesh=mesh, in_specs=placed, out_specs=P(("seq", "head"), None), check_vma=False
    )
```

```python
import functools
import math

import jax
import jax.numpy as jnp
from jax import lax
from jax.experimental import pallas as pl
from jax.experimental.pallas import tpu as pltpu
from jax.sharding import PartitionSpec as P

HEAD_DIM = 128
KEY_ROWS = 512
DOC_MOST = 3584
NEG_START = -1e30


def flash_kernel(meta_ref, doc_ref, q_ref, kt_ref, v_ref, qdoc_ref, kdoc_ref, o_ref, m_sc, l_sc, acc_sc,
                 *, heads_per, groups, q_rows, steps, scale):
    step = pl.program_id(0)
    first_block = meta_ref[0]
    last_block = meta_ref[1]
    q_off = meta_ref[2]
    key_block = jnp.minimum(first_block + step, last_block)
    active = first_block + step <= last_block
    full = (key_block * KEY_ROWS + KEY_ROWS - 1 < q_off) & (
        doc_ref[key_block * KEY_ROWS] == doc_ref[q_off + q_rows - 1]
    )

    @pl.when(step == 0)
    def _():
        m_sc[...] = jnp.full(m_sc.shape, NEG_START, jnp.float32)
        l_sc[...] = jnp.zeros(l_sc.shape, jnp.float32)
        acc_sc[...] = jnp.zeros(acc_sc.shape, jnp.float32)

    def compute(masked):
        if masked:
            query_pos = q_off + lax.broadcasted_iota(jnp.int32, (q_rows, KEY_ROWS), 0)
            key_pos = key_block * KEY_ROWS + lax.broadcasted_iota(jnp.int32, (q_rows, KEY_ROWS), 1)
            visible = (key_pos <= query_pos) & (kdoc_ref[...] == qdoc_ref[...])
        for g in range(groups):
            keys_t = kt_ref[g * HEAD_DIM:(g + 1) * HEAD_DIM, :]
            values = v_ref[:, g * HEAD_DIM:(g + 1) * HEAD_DIM]
            for r in range(heads_per):
                j = g * heads_per + r
                cols = slice(j * HEAD_DIM, (j + 1) * HEAD_DIM)
                scores = jnp.dot(q_ref[:, cols], keys_t, preferred_element_type=jnp.float32)
                if masked:
                    scores = jnp.where(visible, scores, -jnp.inf)
                m_old = m_sc[j]
                m_new = jnp.maximum(m_old, jnp.max(scores, axis=-1, keepdims=True))
                weights = jnp.exp2((scores - m_new) * scale)
                factor = jnp.exp2((m_old - m_new) * scale)
                l_sc[j] = l_sc[j] * factor + jnp.sum(weights, axis=-1, keepdims=True)
                product = jnp.dot(weights.astype(jnp.bfloat16), values, preferred_element_type=jnp.float32)
                acc_sc[:, cols] = acc_sc[:, cols] * factor + product
                m_sc[j] = m_new

    @pl.when(active & full)
    def _():
        compute(False)

    @pl.when(active & jnp.logical_not(full))
    def _():
        compute(True)

    @pl.when(step == steps - 1)
    def _():
        for j in range(groups * heads_per):
            cols = slice(j * HEAD_DIM, (j + 1) * HEAD_DIM)
            o_ref[:, cols] = (acc_sc[:, cols] / l_sc[j]).astype(o_ref.dtype)


def attend(q_tile, q_off, keys_t, values, doc_ids, groups, heads_per):
    tokens = doc_ids.shape[0]
    q_rows = q_tile.shape[0]
    blocks = tokens // KEY_ROWS
    steps = min(blocks, -(-DOC_MOST // KEY_ROWS) + 1)
    doc_start = jnp.sum((doc_ids < doc_ids[q_off]).astype(jnp.int32))
    meta = jnp.stack([doc_start // KEY_ROWS, (q_off + q_rows - 1) // KEY_ROWS, q_off]).astype(jnp.int32)
    width = groups * heads_per * HEAD_DIM
    kv_width = groups * HEAD_DIM

    def key_index(j, meta, docs):
        return jnp.minimum(meta[0] + j, meta[1])

    kernel = functools.partial(
        flash_kernel, heads_per=heads_per, groups=groups, q_rows=q_rows, steps=steps,
        scale=math.log2(math.e) / HEAD_DIM**0.5,
    )
    return pl.pallas_call(
        kernel,
        out_shape=jax.ShapeDtypeStruct((q_rows, width), jnp.bfloat16),
        grid_spec=pltpu.PrefetchScalarGridSpec(
            num_scalar_prefetch=2,
            grid=(steps,),
            in_specs=[
                pl.BlockSpec((q_rows, width), lambda j, meta, docs: (0, 0)),
                pl.BlockSpec((kv_width, KEY_ROWS), lambda j, meta, docs: (0, key_index(j, meta, docs))),
                pl.BlockSpec((KEY_ROWS, kv_width), lambda j, meta, docs: (key_index(j, meta, docs), 0)),
                pl.BlockSpec((q_rows, 1), lambda j, meta, docs: (meta[2] // q_rows, 0)),
                pl.BlockSpec((1, KEY_ROWS), lambda j, meta, docs: (0, key_index(j, meta, docs))),
            ],
            out_specs=pl.BlockSpec((q_rows, width), lambda j, meta, docs: (0, 0)),
            scratch_shapes=[
                pltpu.VMEM((groups * heads_per, q_rows, 1), jnp.float32),
                pltpu.VMEM((groups * heads_per, q_rows, 1), jnp.float32),
                pltpu.VMEM((q_rows, width), jnp.float32),
            ],
        ),
        compiler_params=pltpu.CompilerParams(dimension_semantics=("arbitrary",)),
    )(meta, doc_ids, q_tile, keys_t, values, doc_ids.reshape(tokens, 1), doc_ids.reshape(1, tokens))


def gather_kv(key_rows, value_rows):
    stacked = jnp.stack([key_rows, value_rows], axis=1)
    local = lax.all_to_all(stacked, "head", split_axis=2, concat_axis=0, tiled=True)
    whole = lax.all_gather(local, "seq", axis=0, tiled=True)
    return whole[:, 0, :].T, whole[:, 1, :]


def body(query_rows, key_rows, value_rows, doc_ids):
    head_count = lax.axis_size("head")
    head = lax.axis_index("head")
    sub = query_rows.shape[0]
    q_width = query_rows.shape[1] // head_count
    groups = key_rows.shape[1] // HEAD_DIM // head_count
    heads_per = query_rows.shape[1] // key_rows.shape[1]
    block_start = lax.axis_index("seq") * sub * head_count
    keys_t, values = gather_kv(key_rows, value_rows)
    result = jnp.zeros_like(query_rows)
    for t in range(head_count):
        piece = lax.dynamic_slice_in_dim(query_rows, ((head + t) % head_count) * q_width, q_width, axis=1)
        if t:
            piece = lax.ppermute(piece, "head", [(i, (i + t) % head_count) for i in range(head_count)])
        q_off = block_start + ((head - t) % head_count) * sub
        out_tile = attend(piece, q_off, keys_t, values, doc_ids, groups, heads_per)
        if t:
            out_tile = lax.ppermute(out_tile, "head", [(i, (i - t) % head_count) for i in range(head_count)])
        result = lax.dynamic_update_slice_in_dim(result, out_tile, ((head + t) % head_count) * q_width, axis=1)
    return result


def solution(mesh):
    placed = (P(("seq", "head"), None), P(("seq", "head"), None), P(("seq", "head"), None), P())
    return jax.shard_map(
        body, mesh=mesh, in_specs=placed, out_specs=P(("seq", "head"), None), check_vma=False
    )
```

```python
import functools
import math

import jax
import jax.numpy as jnp
from jax import lax
from jax.experimental import pallas as pl
from jax.experimental.pallas import tpu as pltpu
from jax.sharding import PartitionSpec as P

HEAD_DIM = 128
KEY_ROWS = 512
DOC_MOST = 3584
NEG_START = -1e30


def flash_kernel(meta_ref, doc_ref, q_ref, k_ref, vt_ref, qdoc_ref, kdoc_ref, o_ref, qt_sc, m_sc, l_sc, acc_sc,
                 *, heads_per, groups, q_rows, steps, scale):
    step = pl.program_id(0)
    first_block = meta_ref[0]
    last_block = meta_ref[1]
    q_off = meta_ref[2]
    key_block = jnp.minimum(first_block + step, last_block)
    active = first_block + step <= last_block
    full = (key_block * KEY_ROWS + KEY_ROWS - 1 < q_off) & (
        doc_ref[key_block * KEY_ROWS] == doc_ref[q_off + q_rows - 1]
    )

    @pl.when(step == 0)
    def _():
        m_sc[...] = jnp.full(m_sc.shape, NEG_START, jnp.float32)
        l_sc[...] = jnp.zeros(l_sc.shape, jnp.float32)
        acc_sc[...] = jnp.zeros(acc_sc.shape, jnp.float32)
        for j in range(groups * heads_per):
            cols = slice(j * HEAD_DIM, (j + 1) * HEAD_DIM)
            qt_sc[j] = q_ref[:, cols].astype(jnp.float32).T.astype(jnp.bfloat16)

    def compute(masked):
        if masked:
            key_pos = key_block * KEY_ROWS + lax.broadcasted_iota(jnp.int32, (KEY_ROWS, q_rows), 0)
            query_pos = q_off + lax.broadcasted_iota(jnp.int32, (KEY_ROWS, q_rows), 1)
            visible = (key_pos <= query_pos) & (kdoc_ref[...] == qdoc_ref[0])
        for g in range(groups):
            keys = k_ref[:, g * HEAD_DIM:(g + 1) * HEAD_DIM]
            values_t = vt_ref[g * HEAD_DIM:(g + 1) * HEAD_DIM, :]
            for r in range(heads_per):
                j = g * heads_per + r
                scores = jnp.dot(keys, qt_sc[j], preferred_element_type=jnp.float32)
                if masked:
                    scores = jnp.where(visible, scores, -jnp.inf)
                m_old = m_sc[j]
                m_new = jnp.maximum(m_old, jnp.max(scores, axis=0, keepdims=True))
                weights = jnp.exp2((scores - m_new) * scale)
                factor = jnp.exp2((m_old - m_new) * scale)
                l_sc[j] = l_sc[j] * factor + jnp.sum(weights, axis=0, keepdims=True)
                product = jnp.dot(values_t, weights.astype(jnp.bfloat16), preferred_element_type=jnp.float32)
                acc_sc[j] = acc_sc[j] * factor + product
                m_sc[j] = m_new

    @pl.when(active & full)
    def _():
        compute(False)

    @pl.when(active & jnp.logical_not(full))
    def _():
        compute(True)

    @pl.when(step == steps - 1)
    def _():
        for j in range(groups * heads_per):
            cols = slice(j * HEAD_DIM, (j + 1) * HEAD_DIM)
            o_ref[:, cols] = (acc_sc[j] / l_sc[j]).T.astype(o_ref.dtype)


def attend(q_tile, q_off, keys, values_t, doc_ids, groups, heads_per):
    tokens = doc_ids.shape[0]
    q_rows = q_tile.shape[0]
    blocks = tokens // KEY_ROWS
    steps = min(blocks, -(-DOC_MOST // KEY_ROWS) + 1)
    doc_start = jnp.sum((doc_ids < doc_ids[q_off]).astype(jnp.int32))
    meta = jnp.stack([doc_start // KEY_ROWS, (q_off + q_rows - 1) // KEY_ROWS, q_off]).astype(jnp.int32)
    width = groups * heads_per * HEAD_DIM
    kv_width = groups * HEAD_DIM
    heads = groups * heads_per

    def key_index(j, meta, docs):
        return jnp.minimum(meta[0] + j, meta[1])

    kernel = functools.partial(
        flash_kernel, heads_per=heads_per, groups=groups, q_rows=q_rows, steps=steps,
        scale=math.log2(math.e) / HEAD_DIM**0.5,
    )
    return pl.pallas_call(
        kernel,
        out_shape=jax.ShapeDtypeStruct((q_rows, width), jnp.bfloat16),
        grid_spec=pltpu.PrefetchScalarGridSpec(
            num_scalar_prefetch=2,
            grid=(steps,),
            in_specs=[
                pl.BlockSpec((q_rows, width), lambda j, meta, docs: (0, 0)),
                pl.BlockSpec((KEY_ROWS, kv_width), lambda j, meta, docs: (key_index(j, meta, docs), 0)),
                pl.BlockSpec((kv_width, KEY_ROWS), lambda j, meta, docs: (0, key_index(j, meta, docs))),
                pl.BlockSpec((1, 1, q_rows), lambda j, meta, docs: (meta[2] // q_rows, 0, 0)),
                pl.BlockSpec((KEY_ROWS, 1), lambda j, meta, docs: (key_index(j, meta, docs), 0)),
            ],
            out_specs=pl.BlockSpec((q_rows, width), lambda j, meta, docs: (0, 0)),
            scratch_shapes=[
                pltpu.VMEM((heads, HEAD_DIM, q_rows), jnp.bfloat16),
                pltpu.VMEM((heads, 1, q_rows), jnp.float32),
                pltpu.VMEM((heads, 1, q_rows), jnp.float32),
                pltpu.VMEM((heads, HEAD_DIM, q_rows), jnp.float32),
            ],
        ),
        compiler_params=pltpu.CompilerParams(dimension_semantics=("arbitrary",)),
    )(meta, doc_ids, q_tile, keys, values_t, doc_ids.reshape(tokens // q_rows, 1, q_rows), doc_ids.reshape(tokens, 1))


def gather_kv(key_rows, value_rows):
    stacked = jnp.stack([key_rows, value_rows], axis=1)
    local = lax.all_to_all(stacked, "head", split_axis=2, concat_axis=0, tiled=True)
    whole = lax.all_gather(local, "seq", axis=0, tiled=True)
    return whole[:, 0, :], whole[:, 1, :].T


def body(query_rows, key_rows, value_rows, doc_ids):
    head_count = lax.axis_size("head")
    head = lax.axis_index("head")
    sub = query_rows.shape[0]
    q_width = query_rows.shape[1] // head_count
    groups = key_rows.shape[1] // HEAD_DIM // head_count
    heads_per = query_rows.shape[1] // key_rows.shape[1]
    block_start = lax.axis_index("seq") * sub * head_count
    keys, values_t = gather_kv(key_rows, value_rows)
    result = jnp.zeros_like(query_rows)
    for t in range(head_count):
        piece = lax.dynamic_slice_in_dim(query_rows, ((head + t) % head_count) * q_width, q_width, axis=1)
        if t:
            piece = lax.ppermute(piece, "head", [(i, (i + t) % head_count) for i in range(head_count)])
        q_off = block_start + ((head - t) % head_count) * sub
        out_tile = attend(piece, q_off, keys, values_t, doc_ids, groups, heads_per)
        if t:
            out_tile = lax.ppermute(out_tile, "head", [(i, (i - t) % head_count) for i in range(head_count)])
        result = lax.dynamic_update_slice_in_dim(result, out_tile, ((head + t) % head_count) * q_width, axis=1)
    return result


def solution(mesh):
    placed = (P(("seq", "head"), None), P(("seq", "head"), None), P(("seq", "head"), None), P())
    return jax.shard_map(
        body, mesh=mesh, in_specs=placed, out_specs=P(("seq", "head"), None), check_vma=False
    )
```

```python
import functools
import math

import jax
import jax.numpy as jnp
from jax import lax
from jax.experimental import pallas as pl
from jax.experimental.pallas import tpu as pltpu
from jax.sharding import PartitionSpec as P

HEAD_DIM = 128
KEY_ROWS = 512
DOC_MOST = 3584
NEG_START = -1e30


def flash_kernel(meta_ref, doc_ref, q_ref, k_ref, vt_ref, qstart_ref, o_ref, qt_sc, m_sc, l_sc, acc_sc,
                 *, heads_per, groups, q_rows, steps, scale):
    step = pl.program_id(0)
    first_block = meta_ref[0]
    last_block = meta_ref[1]
    q_off = meta_ref[2]
    key_block = jnp.minimum(first_block + step, last_block)
    active = first_block + step <= last_block
    full = (key_block * KEY_ROWS + KEY_ROWS - 1 < q_off) & (
        doc_ref[key_block * KEY_ROWS] == doc_ref[q_off + q_rows - 1]
    )

    @pl.when(step == 0)
    def _():
        m_sc[...] = jnp.full(m_sc.shape, NEG_START, jnp.float32)
        l_sc[...] = jnp.zeros(l_sc.shape, jnp.float32)
        acc_sc[...] = jnp.zeros(acc_sc.shape, jnp.float32)
        for j in range(groups * heads_per):
            cols = slice(j * HEAD_DIM, (j + 1) * HEAD_DIM)
            qt_sc[j] = q_ref[:, cols].astype(jnp.float32).T.astype(jnp.bfloat16)

    def compute(masked):
        if masked:
            key_pos = key_block * KEY_ROWS + lax.broadcasted_iota(jnp.int32, (KEY_ROWS, q_rows), 0)
            query_pos = q_off + lax.broadcasted_iota(jnp.int32, (KEY_ROWS, q_rows), 1)
            visible = (key_pos <= query_pos) & (key_pos >= qstart_ref[...])
        for g in range(groups):
            keys = k_ref[:, g * HEAD_DIM:(g + 1) * HEAD_DIM]
            values_t = vt_ref[g * HEAD_DIM:(g + 1) * HEAD_DIM, :]
            for r in range(heads_per):
                j = g * heads_per + r
                scores = jnp.dot(keys, qt_sc[j], preferred_element_type=jnp.float32)
                if masked:
                    scores = jnp.where(visible, scores, -jnp.inf)
                m_old = m_sc[j]
                m_new = jnp.maximum(m_old, jnp.max(scores, axis=0, keepdims=True))
                weights = jnp.exp2((scores - m_new) * scale)
                factor = jnp.exp2((m_old - m_new) * scale)
                l_sc[j] = l_sc[j] * factor + jnp.sum(weights, axis=0, keepdims=True)
                product = jnp.dot(values_t, weights.astype(jnp.bfloat16), preferred_element_type=jnp.float32)
                acc_sc[j] = acc_sc[j] * factor + product
                m_sc[j] = m_new

    @pl.when(active & full)
    def _():
        compute(False)

    @pl.when(active & jnp.logical_not(full))
    def _():
        compute(True)

    @pl.when(step == steps - 1)
    def _():
        for j in range(groups * heads_per):
            cols = slice(j * HEAD_DIM, (j + 1) * HEAD_DIM)
            o_ref[:, cols] = (acc_sc[j] / l_sc[j]).T.astype(o_ref.dtype)


def attend(q_tile, q_off, keys, values_t, doc_ids, groups, heads_per):
    tokens = doc_ids.shape[0]
    q_rows = q_tile.shape[0]
    blocks = tokens // KEY_ROWS
    steps = min(blocks, -(-DOC_MOST // KEY_ROWS) + 1)
    query_doc = lax.dynamic_slice_in_dim(doc_ids, q_off, q_rows)
    query_start = jnp.sum((doc_ids[None, :] < query_doc[:, None]).astype(jnp.int32), axis=1).reshape(1, q_rows)
    meta = jnp.stack([query_start[0, 0] // KEY_ROWS, (q_off + q_rows - 1) // KEY_ROWS, q_off]).astype(jnp.int32)
    width = groups * heads_per * HEAD_DIM
    kv_width = groups * HEAD_DIM
    heads = groups * heads_per

    def key_index(j, meta, docs):
        return jnp.minimum(meta[0] + j, meta[1])

    kernel = functools.partial(
        flash_kernel, heads_per=heads_per, groups=groups, q_rows=q_rows, steps=steps,
        scale=math.log2(math.e) / HEAD_DIM**0.5,
    )
    return pl.pallas_call(
        kernel,
        out_shape=jax.ShapeDtypeStruct((q_rows, width), jnp.bfloat16),
        grid_spec=pltpu.PrefetchScalarGridSpec(
            num_scalar_prefetch=2,
            grid=(steps,),
            in_specs=[
                pl.BlockSpec((q_rows, width), lambda j, meta, docs: (0, 0)),
                pl.BlockSpec((KEY_ROWS, kv_width), lambda j, meta, docs: (key_index(j, meta, docs), 0)),
                pl.BlockSpec((kv_width, KEY_ROWS), lambda j, meta, docs: (0, key_index(j, meta, docs))),
                pl.BlockSpec((1, q_rows), lambda j, meta, docs: (0, 0)),
            ],
            out_specs=pl.BlockSpec((q_rows, width), lambda j, meta, docs: (0, 0)),
            scratch_shapes=[
                pltpu.VMEM((heads, HEAD_DIM, q_rows), jnp.bfloat16),
                pltpu.VMEM((heads, 1, q_rows), jnp.float32),
                pltpu.VMEM((heads, 1, q_rows), jnp.float32),
                pltpu.VMEM((heads, HEAD_DIM, q_rows), jnp.float32),
            ],
        ),
        compiler_params=pltpu.CompilerParams(dimension_semantics=("arbitrary",)),
    )(meta, doc_ids, q_tile, keys, values_t, query_start)


def gather_kv(key_rows, value_rows):
    head_count = lax.axis_size("head")
    head = lax.axis_index("head")
    sub = key_rows.shape[0]
    width = key_rows.shape[1] // head_count
    stacked = jnp.stack([key_rows, value_rows], axis=1)
    local = jnp.zeros((head_count * sub, 2, width), stacked.dtype)
    for t in range(head_count):
        piece = lax.dynamic_slice_in_dim(stacked, ((head + t) % head_count) * width, width, axis=2)
        if t:
            piece = lax.ppermute(piece, "head", [(i, (i + t) % head_count) for i in range(head_count)])
        local = lax.dynamic_update_slice_in_dim(local, piece, ((head - t) % head_count) * sub, axis=0)
    whole = lax.all_gather(local, "seq", axis=0, tiled=True)
    return whole[:, 0, :], whole[:, 1, :].T


def body(query_rows, key_rows, value_rows, doc_ids):
    head_count = lax.axis_size("head")
    head = lax.axis_index("head")
    sub = query_rows.shape[0]
    q_width = query_rows.shape[1] // head_count
    groups = key_rows.shape[1] // HEAD_DIM // head_count
    heads_per = query_rows.shape[1] // key_rows.shape[1]
    block_start = lax.axis_index("seq") * sub * head_count
    keys, values_t = gather_kv(key_rows, value_rows)
    result = jnp.zeros_like(query_rows)
    for t in range(head_count):
        piece = lax.dynamic_slice_in_dim(query_rows, ((head + t) % head_count) * q_width, q_width, axis=1)
        if t:
            piece = lax.ppermute(piece, "head", [(i, (i + t) % head_count) for i in range(head_count)])
        q_off = block_start + ((head - t) % head_count) * sub
        out_tile = attend(piece, q_off, keys, values_t, doc_ids, groups, heads_per)
        if t:
            out_tile = lax.ppermute(out_tile, "head", [(i, (i - t) % head_count) for i in range(head_count)])
        result = lax.dynamic_update_slice_in_dim(result, out_tile, ((head + t) % head_count) * q_width, axis=1)
    return result


def solution(mesh):
    placed = (P(("seq", "head"), None), P(("seq", "head"), None), P(("seq", "head"), None), P())
    return jax.shard_map(
        body, mesh=mesh, in_specs=placed, out_specs=P(("seq", "head"), None), check_vma=False
    )
```

```python
import functools
import math

import jax
import jax.numpy as jnp
from jax import lax
from jax.experimental import pallas as pl
from jax.experimental.pallas import tpu as pltpu
from jax.sharding import PartitionSpec as P

HEAD_DIM = 128
KEY_ROWS = 512
DOC_MOST = 3584
WINDOW_BLOCKS = -(-DOC_MOST // KEY_ROWS) + 1
NEG_START = -1e30


def flash_kernel(meta_ref, doc_ref, q_ref, k_ref, vt_ref, qstart_ref, o_ref, qt_sc, m_sc, l_sc, acc_sc,
                 *, heads_per, groups, q_rows, steps, scale):
    step = pl.program_id(0)
    first_block = meta_ref[0]
    last_block = meta_ref[1]
    q_off = meta_ref[2]
    key_block = jnp.minimum(first_block + step, last_block)
    active = first_block + step <= last_block
    full = (key_block * KEY_ROWS + KEY_ROWS - 1 < q_off) & (
        doc_ref[key_block * KEY_ROWS] == doc_ref[q_off + q_rows - 1]
    )

    @pl.when(step == 0)
    def _():
        m_sc[...] = jnp.full(m_sc.shape, NEG_START, jnp.float32)
        l_sc[...] = jnp.zeros(l_sc.shape, jnp.float32)
        acc_sc[...] = jnp.zeros(acc_sc.shape, jnp.float32)
        for j in range(groups * heads_per):
            cols = slice(j * HEAD_DIM, (j + 1) * HEAD_DIM)
            qt_sc[j] = q_ref[:, cols].astype(jnp.float32).T.astype(jnp.bfloat16)

    def compute(masked):
        if masked:
            key_pos = key_block * KEY_ROWS + lax.broadcasted_iota(jnp.int32, (KEY_ROWS, q_rows), 0)
            query_pos = q_off + lax.broadcasted_iota(jnp.int32, (KEY_ROWS, q_rows), 1)
            visible = (key_pos <= query_pos) & (key_pos >= qstart_ref[...])
        for g in range(groups):
            keys = k_ref[:, g * HEAD_DIM:(g + 1) * HEAD_DIM]
            values_t = vt_ref[g * HEAD_DIM:(g + 1) * HEAD_DIM, :]
            for r in range(heads_per):
                j = g * heads_per + r
                scores = jnp.dot(keys, qt_sc[j], preferred_element_type=jnp.float32)
                if masked:
                    scores = jnp.where(visible, scores, -jnp.inf)
                m_old = m_sc[j]
                m_new = jnp.maximum(m_old, jnp.max(scores, axis=0, keepdims=True))
                weights = jnp.exp2((scores - m_new) * scale)
                factor = jnp.exp2((m_old - m_new) * scale)
                l_sc[j] = l_sc[j] * factor + jnp.sum(weights, axis=0, keepdims=True)
                product = jnp.dot(values_t, weights.astype(jnp.bfloat16), preferred_element_type=jnp.float32)
                acc_sc[j] = acc_sc[j] * factor + product
                m_sc[j] = m_new

    @pl.when(active & full)
    def _():
        compute(False)

    @pl.when(active & jnp.logical_not(full))
    def _():
        compute(True)

    @pl.when(step == steps - 1)
    def _():
        for j in range(groups * heads_per):
            cols = slice(j * HEAD_DIM, (j + 1) * HEAD_DIM)
            o_ref[:, cols] = (acc_sc[j] / l_sc[j]).T.astype(o_ref.dtype)


def attend(q_tile, q_off, keys, values_t, doc_ids, groups, heads_per):
    tokens = doc_ids.shape[0]
    q_rows = q_tile.shape[0]
    steps = keys.shape[0]
    query_doc = lax.dynamic_slice_in_dim(doc_ids, q_off, q_rows)
    query_start = jnp.sum((doc_ids[None, :] < query_doc[:, None]).astype(jnp.int32), axis=1).reshape(1, q_rows)
    meta = jnp.stack([query_start[0, 0] // KEY_ROWS, (q_off + q_rows - 1) // KEY_ROWS, q_off]).astype(jnp.int32)
    width = groups * heads_per * HEAD_DIM
    kv_width = groups * HEAD_DIM
    heads = groups * heads_per

    def key_index(j, meta, docs):
        return jnp.minimum(meta[0] + j, meta[1]) - meta[1] + steps - 1

    kernel = functools.partial(
        flash_kernel, heads_per=heads_per, groups=groups, q_rows=q_rows, steps=steps,
        scale=math.log2(math.e) / HEAD_DIM**0.5,
    )
    return pl.pallas_call(
        kernel,
        out_shape=jax.ShapeDtypeStruct((q_rows, width), jnp.bfloat16),
        grid_spec=pltpu.PrefetchScalarGridSpec(
            num_scalar_prefetch=2,
            grid=(steps,),
            in_specs=[
                pl.BlockSpec((q_rows, width), lambda j, meta, docs: (0, 0)),
                pl.BlockSpec((None, KEY_ROWS, kv_width), lambda j, meta, docs: (key_index(j, meta, docs), 0, 0)),
                pl.BlockSpec((None, kv_width, KEY_ROWS), lambda j, meta, docs: (key_index(j, meta, docs), 0, 0)),
                pl.BlockSpec((1, q_rows), lambda j, meta, docs: (0, 0)),
            ],
            out_specs=pl.BlockSpec((q_rows, width), lambda j, meta, docs: (0, 0)),
            scratch_shapes=[
                pltpu.VMEM((heads, HEAD_DIM, q_rows), jnp.bfloat16),
                pltpu.VMEM((heads, 1, q_rows), jnp.float32),
                pltpu.VMEM((heads, 1, q_rows), jnp.float32),
                pltpu.VMEM((heads, HEAD_DIM, q_rows), jnp.float32),
            ],
        ),
        compiler_params=pltpu.CompilerParams(dimension_semantics=("arbitrary",)),
    )(meta, doc_ids, q_tile, keys, values_t, query_start)


def gather_kv(key_rows, value_rows):
    head_count = lax.axis_size("head")
    head = lax.axis_index("head")
    sub = key_rows.shape[0]
    width = key_rows.shape[1] // head_count
    stacked = jnp.stack([key_rows, value_rows], axis=1)
    local = jnp.zeros((head_count * sub, 2, width), stacked.dtype)
    for t in range(head_count):
        piece = lax.dynamic_slice_in_dim(stacked, ((head + t) % head_count) * width, width, axis=2)
        if t:
            piece = lax.ppermute(piece, "head", [(i, (i + t) % head_count) for i in range(head_count)])
        local = lax.dynamic_update_slice_in_dim(local, piece, ((head - t) % head_count) * sub, axis=0)
    seq_count = lax.axis_size("seq")
    window = min(seq_count, WINDOW_BLOCKS)
    slots = [local]
    for d in range(1, window):
        slots.append(lax.ppermute(local, "seq", [(i, i + d) for i in range(seq_count - d)]))
    slots = slots[::-1]
    keys = jnp.stack([slot[:, 0, :] for slot in slots])
    values_t = jnp.stack([slot[:, 1, :].T for slot in slots])
    return keys, values_t


def body(query_rows, key_rows, value_rows, doc_ids):
    head_count = lax.axis_size("head")
    head = lax.axis_index("head")
    sub = query_rows.shape[0]
    q_width = query_rows.shape[1] // head_count
    groups = key_rows.shape[1] // HEAD_DIM // head_count
    heads_per = query_rows.shape[1] // key_rows.shape[1]
    block_start = lax.axis_index("seq") * sub * head_count
    keys, values_t = gather_kv(key_rows, value_rows)
    result = jnp.zeros_like(query_rows)
    for t in range(head_count):
        piece = lax.dynamic_slice_in_dim(query_rows, ((head + t) % head_count) * q_width, q_width, axis=1)
        if t:
            piece = lax.ppermute(piece, "head", [(i, (i + t) % head_count) for i in range(head_count)])
        q_off = block_start + ((head - t) % head_count) * sub
        out_tile = attend(piece, q_off, keys, values_t, doc_ids, groups, heads_per)
        if t:
            out_tile = lax.ppermute(out_tile, "head", [(i, (i - t) % head_count) for i in range(head_count)])
        result = lax.dynamic_update_slice_in_dim(result, out_tile, ((head + t) % head_count) * q_width, axis=1)
    return result


def solution(mesh):
    placed = (P(("seq", "head"), None), P(("seq", "head"), None), P(("seq", "head"), None), P())
    return jax.shard_map(
        body, mesh=mesh, in_specs=placed, out_specs=P(("seq", "head"), None), check_vma=False
    )
```

```python
import functools
import math

import jax
import jax.numpy as jnp
from jax import lax
from jax.experimental import pallas as pl
from jax.experimental.pallas import tpu as pltpu
from jax.sharding import PartitionSpec as P

HEAD_DIM = 128
KEY_ROWS = 512
DOC_MOST = 3584
NEG_START = -1e30


def flash_kernel(meta_ref, doc_ref, q_ref, k_ref, vt_ref, qstart_ref, o_ref, qt_sc, m_sc, l_sc, acc_sc,
                 *, heads_per, groups, q_rows, steps, scale):
    step = pl.program_id(0)
    first_block = meta_ref[0]
    last_block = meta_ref[1]
    q_off = meta_ref[2]
    key_block = jnp.minimum(first_block + step, last_block)
    active = first_block + step <= last_block
    full = (key_block * KEY_ROWS + KEY_ROWS - 1 < q_off) & (
        doc_ref[key_block * KEY_ROWS] == doc_ref[q_off + q_rows - 1]
    )

    @pl.when(step == 0)
    def _():
        m_sc[...] = jnp.full(m_sc.shape, NEG_START, jnp.float32)
        l_sc[...] = jnp.zeros(l_sc.shape, jnp.float32)
        acc_sc[...] = jnp.zeros(acc_sc.shape, jnp.float32)
        for j in range(groups * heads_per):
            cols = slice(j * HEAD_DIM, (j + 1) * HEAD_DIM)
            qt_sc[j] = q_ref[:, cols].astype(jnp.float32).T.astype(jnp.bfloat16)

    def compute(masked):
        if masked:
            key_pos = key_block * KEY_ROWS + lax.broadcasted_iota(jnp.int32, (KEY_ROWS, q_rows), 0)
            query_pos = q_off + lax.broadcasted_iota(jnp.int32, (KEY_ROWS, q_rows), 1)
            visible = (key_pos <= query_pos) & (key_pos >= qstart_ref[...])
        for g in range(groups):
            keys = k_ref[:, g * HEAD_DIM:(g + 1) * HEAD_DIM]
            values_t = vt_ref[g * HEAD_DIM:(g + 1) * HEAD_DIM, :]
            for r in range(heads_per):
                j = g * heads_per + r
                scores = jnp.dot(keys, qt_sc[j], preferred_element_type=jnp.float32)
                if masked:
                    scores = jnp.where(visible, scores, -jnp.inf)
                m_old = m_sc[j]
                m_new = jnp.maximum(m_old, jnp.max(scores, axis=0, keepdims=True))
                weights = jnp.exp2((scores - m_new) * scale)
                factor = jnp.exp2((m_old - m_new) * scale)
                l_sc[j] = l_sc[j] * factor + jnp.sum(weights, axis=0, keepdims=True)
                product = jnp.dot(values_t, weights.astype(jnp.bfloat16), preferred_element_type=jnp.float32)
                acc_sc[j] = acc_sc[j] * factor + product
                m_sc[j] = m_new

    @pl.when(active & full)
    def _():
        compute(False)

    @pl.when(active & jnp.logical_not(full))
    def _():
        compute(True)

    @pl.when(step == steps - 1)
    def _():
        for j in range(groups * heads_per):
            cols = slice(j * HEAD_DIM, (j + 1) * HEAD_DIM)
            o_ref[:, cols] = (acc_sc[j] / l_sc[j]).T.astype(o_ref.dtype)


def attend(q_tile, q_off, keys, values_t, doc_ids, groups, heads_per):
    tokens = doc_ids.shape[0]
    q_rows = q_tile.shape[0]
    blocks = tokens // KEY_ROWS
    steps = min(blocks, -(-DOC_MOST // KEY_ROWS) + 1)
    query_doc = lax.dynamic_slice_in_dim(doc_ids, q_off, q_rows)
    query_start = jnp.sum((doc_ids[None, :] < query_doc[:, None]).astype(jnp.int32), axis=1).reshape(1, q_rows)
    meta = jnp.stack([query_start[0, 0] // KEY_ROWS, (q_off + q_rows - 1) // KEY_ROWS, q_off]).astype(jnp.int32)
    width = groups * heads_per * HEAD_DIM
    kv_width = groups * HEAD_DIM
    heads = groups * heads_per

    def key_index(j, meta, docs):
        return jnp.minimum(meta[0] + j, meta[1])

    kernel = functools.partial(
        flash_kernel, heads_per=heads_per, groups=groups, q_rows=q_rows, steps=steps,
        scale=math.log2(math.e) / HEAD_DIM**0.5,
    )
    return pl.pallas_call(
        kernel,
        out_shape=jax.ShapeDtypeStruct((q_rows, width), jnp.bfloat16),
        grid_spec=pltpu.PrefetchScalarGridSpec(
            num_scalar_prefetch=2,
            grid=(steps,),
            in_specs=[
                pl.BlockSpec((q_rows, width), lambda j, meta, docs: (0, 0)),
                pl.BlockSpec((None, KEY_ROWS, kv_width), lambda j, meta, docs: (key_index(j, meta, docs), 0, 0)),
                pl.BlockSpec((None, kv_width, KEY_ROWS), lambda j, meta, docs: (key_index(j, meta, docs), 0, 0)),
                pl.BlockSpec((1, q_rows), lambda j, meta, docs: (0, 0)),
            ],
            out_specs=pl.BlockSpec((q_rows, width), lambda j, meta, docs: (0, 0)),
            scratch_shapes=[
                pltpu.VMEM((heads, HEAD_DIM, q_rows), jnp.bfloat16),
                pltpu.VMEM((heads, 1, q_rows), jnp.float32),
                pltpu.VMEM((heads, 1, q_rows), jnp.float32),
                pltpu.VMEM((heads, HEAD_DIM, q_rows), jnp.float32),
            ],
        ),
        compiler_params=pltpu.CompilerParams(dimension_semantics=("arbitrary",)),
    )(meta, doc_ids, q_tile, keys, values_t, query_start)


def gather_kv(key_rows, value_rows):
    head_count = lax.axis_size("head")
    head = lax.axis_index("head")
    sub = key_rows.shape[0]
    width = key_rows.shape[1] // head_count
    stacked = jnp.stack([key_rows, value_rows], axis=1)
    local = jnp.zeros((head_count * sub, 2, width), stacked.dtype)
    for t in range(head_count):
        piece = lax.dynamic_slice_in_dim(stacked, ((head + t) % head_count) * width, width, axis=2)
        if t:
            piece = lax.ppermute(piece, "head", [(i, (i + t) % head_count) for i in range(head_count)])
        local = lax.dynamic_update_slice_in_dim(local, piece, ((head - t) % head_count) * sub, axis=0)
    keys = lax.all_gather(local[:, 0, :], "seq", axis=0)
    values_t = lax.all_gather(local[:, 1, :].T, "seq", axis=0)
    return keys, values_t


def body(query_rows, key_rows, value_rows, doc_ids):
    head_count = lax.axis_size("head")
    head = lax.axis_index("head")
    sub = query_rows.shape[0]
    q_width = query_rows.shape[1] // head_count
    groups = key_rows.shape[1] // HEAD_DIM // head_count
    heads_per = query_rows.shape[1] // key_rows.shape[1]
    block_start = lax.axis_index("seq") * sub * head_count
    keys, values_t = gather_kv(key_rows, value_rows)
    result = jnp.zeros_like(query_rows)
    for t in range(head_count):
        piece = lax.dynamic_slice_in_dim(query_rows, ((head + t) % head_count) * q_width, q_width, axis=1)
        if t:
            piece = lax.ppermute(piece, "head", [(i, (i + t) % head_count) for i in range(head_count)])
        q_off = block_start + ((head - t) % head_count) * sub
        out_tile = attend(piece, q_off, keys, values_t, doc_ids, groups, heads_per)
        if t:
            out_tile = lax.ppermute(out_tile, "head", [(i, (i - t) % head_count) for i in range(head_count)])
        result = lax.dynamic_update_slice_in_dim(result, out_tile, ((head + t) % head_count) * q_width, axis=1)
    return result


def solution(mesh):
    placed = (P(("seq", "head"), None), P(("seq", "head"), None), P(("seq", "head"), None), P())
    return jax.shard_map(
        body, mesh=mesh, in_specs=placed, out_specs=P(("seq", "head"), None), check_vma=False
    )
```

```python
import functools
import math

import jax
import jax.numpy as jnp
from jax import lax
from jax.experimental import pallas as pl
from jax.experimental.pallas import tpu as pltpu
from jax.sharding import PartitionSpec as P

HEAD_DIM = 128
KEY_ROWS = 512
DOC_MOST = 3584
NEG_START = -1e30


def flash_kernel(meta_ref, doc_ref, q_ref, k_ref, vt_ref, qstart_ref, o_ref, qt_sc, m_sc, l_sc, acc_sc,
                 *, heads_per, groups, q_rows, steps, scale):
    step = pl.program_id(0)
    first_block = meta_ref[0]
    last_block = meta_ref[1]
    q_off = meta_ref[2]
    key_block = jnp.minimum(first_block + step, last_block)
    active = first_block + step <= last_block
    full = (key_block * KEY_ROWS + KEY_ROWS - 1 < q_off) & (
        doc_ref[key_block * KEY_ROWS] == doc_ref[q_off + q_rows - 1]
    )

    @pl.when(step == 0)
    def _():
        m_sc[...] = jnp.full(m_sc.shape, NEG_START, jnp.float32)
        l_sc[...] = jnp.zeros(l_sc.shape, jnp.float32)
        acc_sc[...] = jnp.zeros(acc_sc.shape, jnp.float32)
        for j in range(groups * heads_per):
            cols = slice(j * HEAD_DIM, (j + 1) * HEAD_DIM)
            qt_sc[j] = q_ref[:, cols].astype(jnp.float32).T.astype(jnp.bfloat16)

    def compute(masked):
        if masked:
            key_pos = key_block * KEY_ROWS + lax.broadcasted_iota(jnp.int32, (KEY_ROWS, q_rows), 0)
            query_pos = q_off + lax.broadcasted_iota(jnp.int32, (KEY_ROWS, q_rows), 1)
            visible = (key_pos <= query_pos) & (key_pos >= qstart_ref[...])
        for g in range(groups):
            keys = k_ref[:, g * HEAD_DIM:(g + 1) * HEAD_DIM]
            values_t = vt_ref[g * HEAD_DIM:(g + 1) * HEAD_DIM, :]
            for r in range(heads_per):
                j = g * heads_per + r
                scores = jnp.dot(keys, qt_sc[j], preferred_element_type=jnp.float32)
                if masked:
                    scores = jnp.where(visible, scores, -jnp.inf)
                m_old = m_sc[j]
                m_new = jnp.maximum(m_old, jnp.max(scores, axis=0, keepdims=True))
                weights = jnp.exp2((scores - m_new) * scale)
                factor = jnp.exp2((m_old - m_new) * scale)
                l_sc[j] = l_sc[j] * factor + jnp.sum(weights, axis=0, keepdims=True)
                product = jnp.dot(values_t, weights.astype(jnp.bfloat16), preferred_element_type=jnp.float32)
                acc_sc[j] = acc_sc[j] * factor + product
                m_sc[j] = m_new

    @pl.when(active & full)
    def _():
        compute(False)

    @pl.when(active & jnp.logical_not(full))
    def _():
        compute(True)

    @pl.when(step == steps - 1)
    def _():
        for j in range(groups * heads_per):
            cols = slice(j * HEAD_DIM, (j + 1) * HEAD_DIM)
            o_ref[:, cols] = (acc_sc[j] / l_sc[j]).T.astype(o_ref.dtype)


def attend(q_tile, q_off, keys, values_t, doc_ids, groups, heads_per):
    tokens = doc_ids.shape[0]
    q_rows = q_tile.shape[0]
    blocks = tokens // KEY_ROWS
    steps = min(blocks, -(-DOC_MOST // KEY_ROWS) + 1)
    query_doc = lax.dynamic_slice_in_dim(doc_ids, q_off, q_rows)
    query_start = jnp.sum((doc_ids[None, :] < query_doc[:, None]).astype(jnp.int32), axis=1).reshape(1, q_rows)
    meta = jnp.stack([query_start[0, 0] // KEY_ROWS, (q_off + q_rows - 1) // KEY_ROWS, q_off]).astype(jnp.int32)
    width = groups * heads_per * HEAD_DIM
    kv_width = groups * HEAD_DIM
    heads = groups * heads_per

    def key_index(j, meta, docs):
        return jnp.minimum(meta[0] + j, meta[1])

    kernel = functools.partial(
        flash_kernel, heads_per=heads_per, groups=groups, q_rows=q_rows, steps=steps,
        scale=math.log2(math.e) / HEAD_DIM**0.5,
    )
    return pl.pallas_call(
        kernel,
        out_shape=jax.ShapeDtypeStruct((q_rows, width), jnp.bfloat16),
        grid_spec=pltpu.PrefetchScalarGridSpec(
            num_scalar_prefetch=2,
            grid=(steps,),
            in_specs=[
                pl.BlockSpec((q_rows, width), lambda j, meta, docs: (0, 0)),
                pl.BlockSpec((KEY_ROWS, kv_width), lambda j, meta, docs: (key_index(j, meta, docs), 0)),
                pl.BlockSpec((kv_width, KEY_ROWS), lambda j, meta, docs: (0, key_index(j, meta, docs))),
                pl.BlockSpec((1, q_rows), lambda j, meta, docs: (0, 0)),
            ],
            out_specs=pl.BlockSpec((q_rows, width), lambda j, meta, docs: (0, 0)),
            scratch_shapes=[
                pltpu.VMEM((heads, HEAD_DIM, q_rows), jnp.bfloat16),
                pltpu.VMEM((heads, 1, q_rows), jnp.float32),
                pltpu.VMEM((heads, 1, q_rows), jnp.float32),
                pltpu.VMEM((heads, HEAD_DIM, q_rows), jnp.float32),
            ],
        ),
        compiler_params=pltpu.CompilerParams(dimension_semantics=("arbitrary",)),
    )(meta, doc_ids, q_tile, keys, values_t, query_start)


def gather_kv(key_rows, value_rows):
    head_count = lax.axis_size("head")
    head = lax.axis_index("head")
    sub = key_rows.shape[0]
    width = key_rows.shape[1] // head_count
    stacked = jnp.stack([key_rows, value_rows], axis=1)
    local = jnp.zeros((head_count * sub, 2, width), stacked.dtype)
    for t in range(head_count):
        piece = lax.dynamic_slice_in_dim(stacked, ((head + t) % head_count) * width, width, axis=2)
        if t:
            piece = lax.ppermute(piece, "head", [(i, (i + t) % head_count) for i in range(head_count)])
        local = lax.dynamic_update_slice_in_dim(local, piece, ((head - t) % head_count) * sub, axis=0)
    seq_count = lax.axis_size("seq")
    copies = jnp.broadcast_to(local[None], (seq_count,) + local.shape).reshape((-1,) + local.shape[1:])
    whole = lax.all_to_all(copies, "seq", split_axis=0, concat_axis=0, tiled=True)
    return whole[:, 0, :], whole[:, 1, :].T


def body(query_rows, key_rows, value_rows, doc_ids):
    head_count = lax.axis_size("head")
    head = lax.axis_index("head")
    sub = query_rows.shape[0]
    q_width = query_rows.shape[1] // head_count
    groups = key_rows.shape[1] // HEAD_DIM // head_count
    heads_per = query_rows.shape[1] // key_rows.shape[1]
    block_start = lax.axis_index("seq") * sub * head_count
    keys, values_t = gather_kv(key_rows, value_rows)
    result = jnp.zeros_like(query_rows)
    for t in range(head_count):
        piece = lax.dynamic_slice_in_dim(query_rows, ((head + t) % head_count) * q_width, q_width, axis=1)
        if t:
            piece = lax.ppermute(piece, "head", [(i, (i + t) % head_count) for i in range(head_count)])
        q_off = block_start + ((head - t) % head_count) * sub
        out_tile = attend(piece, q_off, keys, values_t, doc_ids, groups, heads_per)
        if t:
            out_tile = lax.ppermute(out_tile, "head", [(i, (i - t) % head_count) for i in range(head_count)])
        result = lax.dynamic_update_slice_in_dim(result, out_tile, ((head + t) % head_count) * q_width, axis=1)
    return result


def solution(mesh):
    placed = (P(("seq", "head"), None), P(("seq", "head"), None), P(("seq", "head"), None), P())
    return jax.shard_map(
        body, mesh=mesh, in_specs=placed, out_specs=P(("seq", "head"), None), check_vma=False
    )
```

```python
import functools
import math

import jax
import jax.numpy as jnp
from jax import lax
from jax.experimental import pallas as pl
from jax.experimental.pallas import tpu as pltpu
from jax.sharding import PartitionSpec as P

HEAD_DIM = 128
KEY_ROWS = 512
DOC_MOST = 3584
NEG_START = -1e30


def flash_kernel(meta_ref, doc_ref, q_ref, k_ref, vt_ref, qstart_ref, o_ref, qt_sc, m_sc, l_sc, acc_sc,
                 *, heads_per, groups, q_rows, steps, scale):
    step = pl.program_id(0)
    first_block = meta_ref[0]
    last_block = meta_ref[1]
    q_off = meta_ref[2]
    key_block = jnp.minimum(first_block + step, last_block)
    active = first_block + step <= last_block
    full = (key_block * KEY_ROWS + KEY_ROWS - 1 < q_off) & (
        doc_ref[key_block * KEY_ROWS] == doc_ref[q_off + q_rows - 1]
    )

    @pl.when(step == 0)
    def _():
        m_sc[...] = jnp.full(m_sc.shape, NEG_START, jnp.float32)
        l_sc[...] = jnp.zeros(l_sc.shape, jnp.float32)
        acc_sc[...] = jnp.zeros(acc_sc.shape, jnp.float32)
        for j in range(groups * heads_per):
            cols = slice(j * HEAD_DIM, (j + 1) * HEAD_DIM)
            qt_sc[j] = q_ref[:, cols].astype(jnp.float32).T.astype(jnp.bfloat16)

    def compute(masked):
        if masked:
            key_pos = key_block * KEY_ROWS + lax.broadcasted_iota(jnp.int32, (KEY_ROWS, q_rows), 0)
            query_pos = q_off + lax.broadcasted_iota(jnp.int32, (KEY_ROWS, q_rows), 1)
            visible = (key_pos <= query_pos) & (key_pos >= qstart_ref[...])
        for g in range(groups):
            keys = k_ref[:, g * HEAD_DIM:(g + 1) * HEAD_DIM]
            values_t = vt_ref[g * HEAD_DIM:(g + 1) * HEAD_DIM, :]
            for r in range(heads_per):
                j = g * heads_per + r
                scores = jnp.dot(keys, qt_sc[j], preferred_element_type=jnp.float32)
                if masked:
                    scores = jnp.where(visible, scores, -jnp.inf)
                m_old = m_sc[j]
                m_new = jnp.maximum(m_old, jnp.max(scores, axis=0, keepdims=True))
                weights = jnp.exp2((scores - m_new) * scale)
                factor = jnp.exp2((m_old - m_new) * scale)
                l_sc[j] = l_sc[j] * factor + jnp.sum(weights, axis=0, keepdims=True)
                product = jnp.dot(values_t, weights.astype(jnp.bfloat16), preferred_element_type=jnp.float32)
                acc_sc[j] = acc_sc[j] * factor + product
                m_sc[j] = m_new

    @pl.when(active & full)
    def _():
        compute(False)

    @pl.when(active & jnp.logical_not(full))
    def _():
        compute(True)

    @pl.when(step == steps - 1)
    def _():
        for j in range(groups * heads_per):
            cols = slice(j * HEAD_DIM, (j + 1) * HEAD_DIM)
            o_ref[:, cols] = (acc_sc[j] / l_sc[j]).T.astype(o_ref.dtype)


def attend(q_tile, q_off, keys, values_t, doc_ids, groups, heads_per):
    tokens = doc_ids.shape[0]
    q_rows = q_tile.shape[0]
    blocks = tokens // KEY_ROWS
    steps = min(blocks, -(-DOC_MOST // KEY_ROWS) + 1)
    query_doc = lax.dynamic_slice_in_dim(doc_ids, q_off, q_rows)
    query_start = jnp.sum((doc_ids[None, :] < query_doc[:, None]).astype(jnp.int32), axis=1).reshape(1, q_rows)
    meta = jnp.stack([query_start[0, 0] // KEY_ROWS, (q_off + q_rows - 1) // KEY_ROWS, q_off]).astype(jnp.int32)
    width = groups * heads_per * HEAD_DIM
    kv_width = groups * HEAD_DIM
    heads = groups * heads_per

    def key_index(j, meta, docs):
        return jnp.minimum(meta[0] + j, meta[1])

    kernel = functools.partial(
        flash_kernel, heads_per=heads_per, groups=groups, q_rows=q_rows, steps=steps,
        scale=math.log2(math.e) / HEAD_DIM**0.5,
    )
    return pl.pallas_call(
        kernel,
        out_shape=jax.ShapeDtypeStruct((q_rows, width), jnp.bfloat16),
        grid_spec=pltpu.PrefetchScalarGridSpec(
            num_scalar_prefetch=2,
            grid=(steps,),
            in_specs=[
                pl.BlockSpec((q_rows, width), lambda j, meta, docs: (0, 0)),
                pl.BlockSpec((KEY_ROWS, kv_width), lambda j, meta, docs: (key_index(j, meta, docs), 0)),
                pl.BlockSpec((kv_width, KEY_ROWS), lambda j, meta, docs: (0, key_index(j, meta, docs))),
                pl.BlockSpec((1, q_rows), lambda j, meta, docs: (0, 0)),
            ],
            out_specs=pl.BlockSpec((q_rows, width), lambda j, meta, docs: (0, 0)),
            scratch_shapes=[
                pltpu.VMEM((heads, HEAD_DIM, q_rows), jnp.bfloat16),
                pltpu.VMEM((heads, 1, q_rows), jnp.float32),
                pltpu.VMEM((heads, 1, q_rows), jnp.float32),
                pltpu.VMEM((heads, HEAD_DIM, q_rows), jnp.float32),
            ],
        ),
        compiler_params=pltpu.CompilerParams(dimension_semantics=("arbitrary",)),
    )(meta, doc_ids, q_tile, keys, values_t, query_start)


def gather_seq(local):
    seq_count = lax.axis_size("seq")
    assert seq_count & (seq_count - 1) == 0
    seq = lax.axis_index("seq")
    rows = local.shape[0]
    whole = jnp.zeros((seq_count * rows,) + local.shape[1:], local.dtype)
    whole = lax.dynamic_update_slice_in_dim(whole, local, seq * rows, axis=0)
    span = 1
    while span < seq_count:
        base = (seq // span) * span
        held = lax.dynamic_slice_in_dim(whole, base * rows, span * rows, axis=0)
        got = lax.ppermute(held, "seq", [(i, i ^ span) for i in range(seq_count)])
        whole = lax.dynamic_update_slice_in_dim(whole, got, (base ^ span) * rows, axis=0)
        span *= 2
    return whole


def gather_kv(key_rows, value_rows):
    head_count = lax.axis_size("head")
    head = lax.axis_index("head")
    sub = key_rows.shape[0]
    width = key_rows.shape[1] // head_count
    stacked = jnp.stack([key_rows, value_rows], axis=1)
    local = jnp.zeros((head_count * sub, 2, width), stacked.dtype)
    for t in range(head_count):
        piece = lax.dynamic_slice_in_dim(stacked, ((head + t) % head_count) * width, width, axis=2)
        if t:
            piece = lax.ppermute(piece, "head", [(i, (i + t) % head_count) for i in range(head_count)])
        local = lax.dynamic_update_slice_in_dim(local, piece, ((head - t) % head_count) * sub, axis=0)
    whole = gather_seq(local)
    return whole[:, 0, :], whole[:, 1, :].T


def body(query_rows, key_rows, value_rows, doc_ids):
    head_count = lax.axis_size("head")
    head = lax.axis_index("head")
    sub = query_rows.shape[0]
    q_width = query_rows.shape[1] // head_count
    groups = key_rows.shape[1] // HEAD_DIM // head_count
    heads_per = query_rows.shape[1] // key_rows.shape[1]
    block_start = lax.axis_index("seq") * sub * head_count
    keys, values_t = gather_kv(key_rows, value_rows)
    result = jnp.zeros_like(query_rows)
    for t in range(head_count):
        piece = lax.dynamic_slice_in_dim(query_rows, ((head + t) % head_count) * q_width, q_width, axis=1)
        if t:
            piece = lax.ppermute(piece, "head", [(i, (i + t) % head_count) for i in range(head_count)])
        q_off = block_start + ((head - t) % head_count) * sub
        out_tile = attend(piece, q_off, keys, values_t, doc_ids, groups, heads_per)
        if t:
            out_tile = lax.ppermute(out_tile, "head", [(i, (i - t) % head_count) for i in range(head_count)])
        result = lax.dynamic_update_slice_in_dim(result, out_tile, ((head + t) % head_count) * q_width, axis=1)
    return result


def solution(mesh):
    placed = (P(("seq", "head"), None), P(("seq", "head"), None), P(("seq", "head"), None), P())
    return jax.shard_map(
        body, mesh=mesh, in_specs=placed, out_specs=P(("seq", "head"), None), check_vma=False
    )
```

```python
import functools
import math

import jax
import jax.numpy as jnp
from jax import lax
from jax.experimental import pallas as pl
from jax.experimental.pallas import tpu as pltpu
from jax.sharding import PartitionSpec as P

HEAD_DIM = 128
KEY_ROWS = 512
DOC_MOST = 3584
NEG_START = -1e30


def flash_kernel(meta_ref, doc_ref, q_ref, k_ref, vt_ref, qstart_ref, o_ref, qt_sc, m_sc, l_sc, acc_sc,
                 *, heads_per, groups, q_rows, steps, scale):
    step = pl.program_id(0)
    first_block = meta_ref[0]
    last_block = meta_ref[1]
    q_off = meta_ref[2]
    key_block = jnp.minimum(first_block + step, last_block)
    active = first_block + step <= last_block
    full = (key_block * KEY_ROWS + KEY_ROWS - 1 < q_off) & (
        doc_ref[key_block * KEY_ROWS] == doc_ref[q_off + q_rows - 1]
    )

    @pl.when(step == 0)
    def _():
        m_sc[...] = jnp.full(m_sc.shape, NEG_START, jnp.float32)
        l_sc[...] = jnp.zeros(l_sc.shape, jnp.float32)
        acc_sc[...] = jnp.zeros(acc_sc.shape, jnp.float32)
        for j in range(groups * heads_per):
            cols = slice(j * HEAD_DIM, (j + 1) * HEAD_DIM)
            qt_sc[j] = q_ref[:, cols].astype(jnp.float32).T.astype(jnp.bfloat16)

    def compute(masked):
        if masked:
            key_pos = key_block * KEY_ROWS + lax.broadcasted_iota(jnp.int32, (KEY_ROWS, q_rows), 0)
            query_pos = q_off + lax.broadcasted_iota(jnp.int32, (KEY_ROWS, q_rows), 1)
            visible = (key_pos <= query_pos) & (key_pos >= qstart_ref[...])
        for g in range(groups):
            keys = k_ref[:, g * HEAD_DIM:(g + 1) * HEAD_DIM]
            values_t = vt_ref[g * HEAD_DIM:(g + 1) * HEAD_DIM, :]
            for r in range(heads_per):
                j = g * heads_per + r
                scores = jnp.dot(keys, qt_sc[j], preferred_element_type=jnp.float32)
                if masked:
                    scores = jnp.where(visible, scores, -jnp.inf)
                m_old = m_sc[j]
                m_new = jnp.maximum(m_old, jnp.max(scores, axis=0, keepdims=True))
                weights = jnp.exp2((scores - m_new) * scale)
                factor = jnp.exp2((m_old - m_new) * scale)
                l_sc[j] = l_sc[j] * factor + jnp.sum(weights, axis=0, keepdims=True)
                product = jnp.dot(values_t, weights.astype(jnp.bfloat16), preferred_element_type=jnp.float32)
                acc_sc[j] = acc_sc[j] * factor + product
                m_sc[j] = m_new

    @pl.when(active & full)
    def _():
        compute(False)

    @pl.when(active & jnp.logical_not(full))
    def _():
        compute(True)

    @pl.when(step == steps - 1)
    def _():
        for j in range(groups * heads_per):
            cols = slice(j * HEAD_DIM, (j + 1) * HEAD_DIM)
            o_ref[:, cols] = (acc_sc[j] / l_sc[j]).T.astype(o_ref.dtype)


def attend(q_tile, q_off, keys, values_t, doc_ids, groups, heads_per):
    tokens = doc_ids.shape[0]
    q_rows = q_tile.shape[0]
    blocks = tokens // KEY_ROWS
    steps = min(blocks, -(-DOC_MOST // KEY_ROWS) + 1)
    query_doc = lax.dynamic_slice_in_dim(doc_ids, q_off, q_rows)
    query_start = jnp.sum((doc_ids[None, :] < query_doc[:, None]).astype(jnp.int32), axis=1).reshape(1, q_rows)
    meta = jnp.stack([query_start[0, 0] // KEY_ROWS, (q_off + q_rows - 1) // KEY_ROWS, q_off]).astype(jnp.int32)
    width = groups * heads_per * HEAD_DIM
    kv_width = groups * HEAD_DIM
    heads = groups * heads_per

    def key_index(j, meta, docs):
        return jnp.minimum(meta[0] + j, meta[1])

    kernel = functools.partial(
        flash_kernel, heads_per=heads_per, groups=groups, q_rows=q_rows, steps=steps,
        scale=math.log2(math.e) / HEAD_DIM**0.5,
    )
    return pl.pallas_call(
        kernel,
        out_shape=jax.ShapeDtypeStruct((q_rows, width), jnp.bfloat16),
        grid_spec=pltpu.PrefetchScalarGridSpec(
            num_scalar_prefetch=2,
            grid=(steps,),
            in_specs=[
                pl.BlockSpec((q_rows, width), lambda j, meta, docs: (0, 0)),
                pl.BlockSpec((KEY_ROWS, kv_width), lambda j, meta, docs: (key_index(j, meta, docs), 0)),
                pl.BlockSpec((kv_width, KEY_ROWS), lambda j, meta, docs: (0, key_index(j, meta, docs))),
                pl.BlockSpec((1, q_rows), lambda j, meta, docs: (0, 0)),
            ],
            out_specs=pl.BlockSpec((q_rows, width), lambda j, meta, docs: (0, 0)),
            scratch_shapes=[
                pltpu.VMEM((heads, HEAD_DIM, q_rows), jnp.bfloat16),
                pltpu.VMEM((heads, 1, q_rows), jnp.float32),
                pltpu.VMEM((heads, 1, q_rows), jnp.float32),
                pltpu.VMEM((heads, HEAD_DIM, q_rows), jnp.float32),
            ],
        ),
        compiler_params=pltpu.CompilerParams(dimension_semantics=("arbitrary",)),
    )(meta, doc_ids, q_tile, keys, values_t, query_start)


def gather_seq(local):
    seq_count = lax.axis_size("seq")
    if seq_count != 8:
        return lax.all_gather(local, "seq", axis=0, tiled=True)
    seq = lax.axis_index("seq")
    chips = seq_count // 2
    core = seq % 2
    mine = jnp.zeros((chips,) + local.shape, local.dtype)
    mine = lax.dynamic_update_index_in_dim(mine, local, seq // 2, axis=0)
    for k in range(1, chips):
        got = lax.ppermute(local, "seq", [(i, i ^ (2 * k)) for i in range(seq_count)])
        mine = lax.dynamic_update_index_in_dim(mine, got, (seq ^ (2 * k)) // 2, axis=0)
    sibling = lax.ppermute(mine, "seq", [(i, i ^ 1) for i in range(seq_count)])
    paired = jnp.zeros((chips, 2) + local.shape, local.dtype)
    paired = lax.dynamic_update_slice_in_dim(paired, mine[:, None], core, axis=1)
    paired = lax.dynamic_update_slice_in_dim(paired, sibling[:, None], 1 - core, axis=1)
    return paired.reshape((seq_count * local.shape[0],) + local.shape[1:])


def gather_kv(key_rows, value_rows):
    head_count = lax.axis_size("head")
    head = lax.axis_index("head")
    sub = key_rows.shape[0]
    width = key_rows.shape[1] // head_count
    stacked = jnp.stack([key_rows, value_rows], axis=1)
    local = jnp.zeros((head_count * sub, 2, width), stacked.dtype)
    for t in range(head_count):
        piece = lax.dynamic_slice_in_dim(stacked, ((head + t) % head_count) * width, width, axis=2)
        if t:
            piece = lax.ppermute(piece, "head", [(i, (i + t) % head_count) for i in range(head_count)])
        local = lax.dynamic_update_slice_in_dim(local, piece, ((head - t) % head_count) * sub, axis=0)
    whole = gather_seq(local)
    return whole[:, 0, :], whole[:, 1, :].T


def body(query_rows, key_rows, value_rows, doc_ids):
    head_count = lax.axis_size("head")
    head = lax.axis_index("head")
    sub = query_rows.shape[0]
    q_width = query_rows.shape[1] // head_count
    groups = key_rows.shape[1] // HEAD_DIM // head_count
    heads_per = query_rows.shape[1] // key_rows.shape[1]
    block_start = lax.axis_index("seq") * sub * head_count
    keys, values_t = gather_kv(key_rows, value_rows)
    result = jnp.zeros_like(query_rows)
    for t in range(head_count):
        piece = lax.dynamic_slice_in_dim(query_rows, ((head + t) % head_count) * q_width, q_width, axis=1)
        if t:
            piece = lax.ppermute(piece, "head", [(i, (i + t) % head_count) for i in range(head_count)])
        q_off = block_start + ((head - t) % head_count) * sub
        out_tile = attend(piece, q_off, keys, values_t, doc_ids, groups, heads_per)
        if t:
            out_tile = lax.ppermute(out_tile, "head", [(i, (i - t) % head_count) for i in range(head_count)])
        result = lax.dynamic_update_slice_in_dim(result, out_tile, ((head + t) % head_count) * q_width, axis=1)
    return result


def solution(mesh):
    placed = (P(("seq", "head"), None), P(("seq", "head"), None), P(("seq", "head"), None), P())
    return jax.shard_map(
        body, mesh=mesh, in_specs=placed, out_specs=P(("seq", "head"), None), check_vma=False
    )
```

```python
import functools
import math

import jax
import jax.numpy as jnp
from jax import lax
from jax.experimental import pallas as pl
from jax.experimental.pallas import tpu as pltpu
from jax.sharding import PartitionSpec as P

HEAD_DIM = 128
KEY_ROWS = 512
DOC_MOST = 3584
NEG_START = -1e30


def flash_kernel(meta_ref, doc_ref, q_ref, k_ref, v_ref, qstart_ref, o_ref, qt_sc, m_sc, l_sc, acc_sc,
                 *, heads_per, groups, q_rows, steps, scale):
    step = pl.program_id(0)
    first_block = meta_ref[0]
    last_block = meta_ref[1]
    q_off = meta_ref[2]
    key_block = jnp.minimum(first_block + step, last_block)
    active = first_block + step <= last_block
    full = (key_block * KEY_ROWS + KEY_ROWS - 1 < q_off) & (
        doc_ref[key_block * KEY_ROWS] == doc_ref[q_off + q_rows - 1]
    )

    @pl.when(step == 0)
    def _():
        m_sc[...] = jnp.full(m_sc.shape, NEG_START, jnp.float32)
        l_sc[...] = jnp.zeros(l_sc.shape, jnp.float32)
        acc_sc[...] = jnp.zeros(acc_sc.shape, jnp.float32)
        for j in range(groups * heads_per):
            cols = slice(j * HEAD_DIM, (j + 1) * HEAD_DIM)
            qt_sc[j] = q_ref[:, cols].astype(jnp.float32).T.astype(jnp.bfloat16)

    def compute(masked):
        if masked:
            key_pos = key_block * KEY_ROWS + lax.broadcasted_iota(jnp.int32, (KEY_ROWS, q_rows), 0)
            query_pos = q_off + lax.broadcasted_iota(jnp.int32, (KEY_ROWS, q_rows), 1)
            visible = (key_pos <= query_pos) & (key_pos >= qstart_ref[...])
        for g in range(groups):
            keys = k_ref[:, g * HEAD_DIM:(g + 1) * HEAD_DIM]
            values_t = v_ref[:, g * HEAD_DIM:(g + 1) * HEAD_DIM].astype(jnp.float32).T.astype(jnp.bfloat16)
            for r in range(heads_per):
                j = g * heads_per + r
                scores = jnp.dot(keys, qt_sc[j], preferred_element_type=jnp.float32)
                if masked:
                    scores = jnp.where(visible, scores, -jnp.inf)
                m_old = m_sc[j]
                m_new = jnp.maximum(m_old, jnp.max(scores, axis=0, keepdims=True))
                weights = jnp.exp2((scores - m_new) * scale)
                factor = jnp.exp2((m_old - m_new) * scale)
                l_sc[j] = l_sc[j] * factor + jnp.sum(weights, axis=0, keepdims=True)
                product = jnp.dot(values_t, weights.astype(jnp.bfloat16), preferred_element_type=jnp.float32)
                acc_sc[j] = acc_sc[j] * factor + product
                m_sc[j] = m_new

    @pl.when(active & full)
    def _():
        compute(False)

    @pl.when(active & jnp.logical_not(full))
    def _():
        compute(True)

    @pl.when(step == steps - 1)
    def _():
        for j in range(groups * heads_per):
            cols = slice(j * HEAD_DIM, (j + 1) * HEAD_DIM)
            o_ref[:, cols] = (acc_sc[j] / l_sc[j]).T.astype(o_ref.dtype)


def attend(q_tile, q_off, kv_rows, doc_ids, groups, heads_per):
    tokens = doc_ids.shape[0]
    q_rows = q_tile.shape[0]
    blocks = tokens // KEY_ROWS
    steps = min(blocks, -(-DOC_MOST // KEY_ROWS) + 1)
    query_doc = lax.dynamic_slice_in_dim(doc_ids, q_off, q_rows)
    query_start = jnp.sum((doc_ids[None, :] < query_doc[:, None]).astype(jnp.int32), axis=1).reshape(1, q_rows)
    meta = jnp.stack([query_start[0, 0] // KEY_ROWS, (q_off + q_rows - 1) // KEY_ROWS, q_off]).astype(jnp.int32)
    width = groups * heads_per * HEAD_DIM
    kv_width = groups * HEAD_DIM
    heads = groups * heads_per

    def key_index(j, meta, docs):
        return jnp.minimum(meta[0] + j, meta[1])

    kernel = functools.partial(
        flash_kernel, heads_per=heads_per, groups=groups, q_rows=q_rows, steps=steps,
        scale=math.log2(math.e) / HEAD_DIM**0.5,
    )
    return pl.pallas_call(
        kernel,
        out_shape=jax.ShapeDtypeStruct((q_rows, width), jnp.bfloat16),
        grid_spec=pltpu.PrefetchScalarGridSpec(
            num_scalar_prefetch=2,
            grid=(steps,),
            in_specs=[
                pl.BlockSpec((q_rows, width), lambda j, meta, docs: (0, 0)),
                pl.BlockSpec((KEY_ROWS, kv_width), lambda j, meta, docs: (key_index(j, meta, docs), 0)),
                pl.BlockSpec((KEY_ROWS, kv_width), lambda j, meta, docs: (key_index(j, meta, docs), 1)),
                pl.BlockSpec((1, q_rows), lambda j, meta, docs: (0, 0)),
            ],
            out_specs=pl.BlockSpec((q_rows, width), lambda j, meta, docs: (0, 0)),
            scratch_shapes=[
                pltpu.VMEM((heads, HEAD_DIM, q_rows), jnp.bfloat16),
                pltpu.VMEM((heads, 1, q_rows), jnp.float32),
                pltpu.VMEM((heads, 1, q_rows), jnp.float32),
                pltpu.VMEM((heads, HEAD_DIM, q_rows), jnp.float32),
            ],
        ),
        compiler_params=pltpu.CompilerParams(dimension_semantics=("arbitrary",)),
    )(meta, doc_ids, q_tile, kv_rows, kv_rows, query_start)


def gather_kv(key_rows, value_rows):
    head_count = lax.axis_size("head")
    head = lax.axis_index("head")
    sub = key_rows.shape[0]
    width = key_rows.shape[1] // head_count
    local = jnp.zeros((head_count * sub, 2 * width), key_rows.dtype)
    for t in range(head_count):
        cols = ((head + t) % head_count) * width
        piece = jnp.concatenate(
            [lax.dynamic_slice_in_dim(key_rows, cols, width, axis=1),
             lax.dynamic_slice_in_dim(value_rows, cols, width, axis=1)], axis=1)
        if t:
            piece = lax.ppermute(piece, "head", [(i, (i + t) % head_count) for i in range(head_count)])
        local = lax.dynamic_update_slice_in_dim(local, piece, ((head - t) % head_count) * sub, axis=0)
    return lax.all_gather(local, "seq", axis=0, tiled=True)


def body(query_rows, key_rows, value_rows, doc_ids):
    head_count = lax.axis_size("head")
    head = lax.axis_index("head")
    sub = query_rows.shape[0]
    q_width = query_rows.shape[1] // head_count
    groups = key_rows.shape[1] // HEAD_DIM // head_count
    heads_per = query_rows.shape[1] // key_rows.shape[1]
    block_start = lax.axis_index("seq") * sub * head_count
    kv_rows = gather_kv(key_rows, value_rows)
    result = jnp.zeros_like(query_rows)
    for t in range(head_count):
        piece = lax.dynamic_slice_in_dim(query_rows, ((head + t) % head_count) * q_width, q_width, axis=1)
        if t:
            piece = lax.ppermute(piece, "head", [(i, (i + t) % head_count) for i in range(head_count)])
        q_off = block_start + ((head - t) % head_count) * sub
        out_tile = attend(piece, q_off, kv_rows, doc_ids, groups, heads_per)
        if t:
            out_tile = lax.ppermute(out_tile, "head", [(i, (i - t) % head_count) for i in range(head_count)])
        result = lax.dynamic_update_slice_in_dim(result, out_tile, ((head + t) % head_count) * q_width, axis=1)
    return result


def solution(mesh):
    placed = (P(("seq", "head"), None), P(("seq", "head"), None), P(("seq", "head"), None), P())
    return jax.shard_map(
        body, mesh=mesh, in_specs=placed, out_specs=P(("seq", "head"), None), check_vma=False
    )
```

```python
import functools
import math

import jax
import jax.numpy as jnp
from jax import lax
from jax.experimental import pallas as pl
from jax.experimental.pallas import tpu as pltpu
from jax.sharding import PartitionSpec as P

HEAD_DIM = 128
KEY_ROWS = 512
DOC_MOST = 3584
NEG_START = -1e30


def flash_kernel(meta_ref, doc_ref, q_ref, k_ref, v_ref, qstart_ref, o_ref, qt_sc, m_sc, l_sc, acc_sc,
                 *, heads_per, groups, q_rows, steps, scale):
    step = pl.program_id(0)
    first_block = meta_ref[0]
    last_block = meta_ref[1]
    q_off = meta_ref[2]
    key_block = jnp.minimum(first_block + step, last_block)
    active = first_block + step <= last_block
    full = (key_block * KEY_ROWS + KEY_ROWS - 1 < q_off) & (
        doc_ref[key_block * KEY_ROWS] == doc_ref[q_off + q_rows - 1]
    )

    @pl.when(step == 0)
    def _():
        m_sc[...] = jnp.full(m_sc.shape, NEG_START, jnp.float32)
        l_sc[...] = jnp.zeros(l_sc.shape, jnp.float32)
        acc_sc[...] = jnp.zeros(acc_sc.shape, jnp.float32)
        for j in range(groups * heads_per):
            cols = slice(j * HEAD_DIM, (j + 1) * HEAD_DIM)
            qt_sc[j] = q_ref[:, cols].astype(jnp.float32).T.astype(jnp.bfloat16)

    def compute(masked):
        if masked:
            key_pos = key_block * KEY_ROWS + lax.broadcasted_iota(jnp.int32, (KEY_ROWS, q_rows), 0)
            query_pos = q_off + lax.broadcasted_iota(jnp.int32, (KEY_ROWS, q_rows), 1)
            visible = (key_pos <= query_pos) & (key_pos >= qstart_ref[...])
        for g in range(groups):
            keys = k_ref[:, g * HEAD_DIM:(g + 1) * HEAD_DIM]
            values_t = v_ref[:, g * HEAD_DIM:(g + 1) * HEAD_DIM].T
            for r in range(heads_per):
                j = g * heads_per + r
                scores = jnp.dot(keys, qt_sc[j], preferred_element_type=jnp.float32)
                if masked:
                    scores = jnp.where(visible, scores, -jnp.inf)
                m_old = m_sc[j]
                m_new = jnp.maximum(m_old, jnp.max(scores, axis=0, keepdims=True))
                weights = jnp.exp2((scores - m_new) * scale)
                factor = jnp.exp2((m_old - m_new) * scale)
                l_sc[j] = l_sc[j] * factor + jnp.sum(weights, axis=0, keepdims=True)
                product = jnp.dot(values_t, weights.astype(jnp.bfloat16), preferred_element_type=jnp.float32)
                acc_sc[j] = acc_sc[j] * factor + product
                m_sc[j] = m_new

    @pl.when(active & full)
    def _():
        compute(False)

    @pl.when(active & jnp.logical_not(full))
    def _():
        compute(True)

    @pl.when(step == steps - 1)
    def _():
        for j in range(groups * heads_per):
            cols = slice(j * HEAD_DIM, (j + 1) * HEAD_DIM)
            o_ref[:, cols] = (acc_sc[j] / l_sc[j]).T.astype(o_ref.dtype)


def attend(q_tile, q_off, kv_rows, doc_ids, groups, heads_per):
    tokens = doc_ids.shape[0]
    q_rows = q_tile.shape[0]
    blocks = tokens // KEY_ROWS
    steps = min(blocks, -(-DOC_MOST // KEY_ROWS) + 1)
    query_doc = lax.dynamic_slice_in_dim(doc_ids, q_off, q_rows)
    query_start = jnp.sum((doc_ids[None, :] < query_doc[:, None]).astype(jnp.int32), axis=1).reshape(1, q_rows)
    meta = jnp.stack([query_start[0, 0] // KEY_ROWS, (q_off + q_rows - 1) // KEY_ROWS, q_off]).astype(jnp.int32)
    width = groups * heads_per * HEAD_DIM
    kv_width = groups * HEAD_DIM
    heads = groups * heads_per

    def key_index(j, meta, docs):
        return jnp.minimum(meta[0] + j, meta[1])

    kernel = functools.partial(
        flash_kernel, heads_per=heads_per, groups=groups, q_rows=q_rows, steps=steps,
        scale=math.log2(math.e) / HEAD_DIM**0.5,
    )
    return pl.pallas_call(
        kernel,
        out_shape=jax.ShapeDtypeStruct((q_rows, width), jnp.bfloat16),
        grid_spec=pltpu.PrefetchScalarGridSpec(
            num_scalar_prefetch=2,
            grid=(steps,),
            in_specs=[
                pl.BlockSpec((q_rows, width), lambda j, meta, docs: (0, 0)),
                pl.BlockSpec((KEY_ROWS, kv_width), lambda j, meta, docs: (key_index(j, meta, docs), 0)),
                pl.BlockSpec((KEY_ROWS, kv_width), lambda j, meta, docs: (key_index(j, meta, docs), 1)),
                pl.BlockSpec((1, q_rows), lambda j, meta, docs: (0, 0)),
            ],
            out_specs=pl.BlockSpec((q_rows, width), lambda j, meta, docs: (0, 0)),
            scratch_shapes=[
                pltpu.VMEM((heads, HEAD_DIM, q_rows), jnp.bfloat16),
                pltpu.VMEM((heads, 1, q_rows), jnp.float32),
                pltpu.VMEM((heads, 1, q_rows), jnp.float32),
                pltpu.VMEM((heads, HEAD_DIM, q_rows), jnp.float32),
            ],
        ),
        compiler_params=pltpu.CompilerParams(dimension_semantics=("arbitrary",)),
    )(meta, doc_ids, q_tile, kv_rows, kv_rows, query_start)


def gather_kv(key_rows, value_rows):
    head_count = lax.axis_size("head")
    head = lax.axis_index("head")
    sub = key_rows.shape[0]
    width = key_rows.shape[1] // head_count
    local = jnp.zeros((head_count * sub, 2 * width), key_rows.dtype)
    for t in range(head_count):
        cols = ((head + t) % head_count) * width
        piece = jnp.concatenate(
            [lax.dynamic_slice_in_dim(key_rows, cols, width, axis=1),
             lax.dynamic_slice_in_dim(value_rows, cols, width, axis=1)], axis=1)
        if t:
            piece = lax.ppermute(piece, "head", [(i, (i + t) % head_count) for i in range(head_count)])
        local = lax.dynamic_update_slice_in_dim(local, piece, ((head - t) % head_count) * sub, axis=0)
    return lax.all_gather(local, "seq", axis=0, tiled=True)


def body(query_rows, key_rows, value_rows, doc_ids):
    head_count = lax.axis_size("head")
    head = lax.axis_index("head")
    sub = query_rows.shape[0]
    q_width = query_rows.shape[1] // head_count
    groups = key_rows.shape[1] // HEAD_DIM // head_count
    heads_per = query_rows.shape[1] // key_rows.shape[1]
    block_start = lax.axis_index("seq") * sub * head_count
    kv_rows = gather_kv(key_rows, value_rows)
    result = jnp.zeros_like(query_rows)
    for t in range(head_count):
        piece = lax.dynamic_slice_in_dim(query_rows, ((head + t) % head_count) * q_width, q_width, axis=1)
        if t:
            piece = lax.ppermute(piece, "head", [(i, (i + t) % head_count) for i in range(head_count)])
        q_off = block_start + ((head - t) % head_count) * sub
        out_tile = attend(piece, q_off, kv_rows, doc_ids, groups, heads_per)
        if t:
            out_tile = lax.ppermute(out_tile, "head", [(i, (i - t) % head_count) for i in range(head_count)])
        result = lax.dynamic_update_slice_in_dim(result, out_tile, ((head + t) % head_count) * q_width, axis=1)
    return result


def solution(mesh):
    placed = (P(("seq", "head"), None), P(("seq", "head"), None), P(("seq", "head"), None), P())
    return jax.shard_map(
        body, mesh=mesh, in_specs=placed, out_specs=P(("seq", "head"), None), check_vma=False
    )
```

```python
import functools
import math

import jax
import jax.numpy as jnp
from jax import lax
from jax.experimental import pallas as pl
from jax.experimental.pallas import tpu as pltpu
from jax.sharding import PartitionSpec as P

HEAD_DIM = 128
KEY_ROWS = 512
DOC_MOST = 3584
NEG_START = -1e30


def flash_kernel(meta_ref, doc_ref, q_ref, ka_ref, va_ref, kb_ref, vb_ref, qstart_ref, o_ref, qt_sc, m_sc, l_sc,
                 acc_sc, *, heads_per, groups, q_rows, steps, scale, sub, head_count):
    step = pl.program_id(0)
    first_block = meta_ref[0]
    last_block = meta_ref[1]
    q_off = meta_ref[2]
    head = meta_ref[3]
    key_block = jnp.minimum(first_block + step, last_block)
    active = first_block + step <= last_block
    full = (key_block * KEY_ROWS + KEY_ROWS - 1 < q_off) & (
        doc_ref[key_block * KEY_ROWS] == doc_ref[q_off + q_rows - 1]
    )

    @pl.when(step == 0)
    def _():
        m_sc[...] = jnp.full(m_sc.shape, NEG_START, jnp.float32)
        l_sc[...] = jnp.zeros(l_sc.shape, jnp.float32)
        acc_sc[...] = jnp.zeros(acc_sc.shape, jnp.float32)
        for j in range(groups * heads_per):
            cols = slice(j * HEAD_DIM, (j + 1) * HEAD_DIM)
            qt_sc[j] = q_ref[:, cols].astype(jnp.float32).T.astype(jnp.bfloat16)

    def compute(masked):
        parts = [(ka_ref, va_ref), (kb_ref, vb_ref)]
        if masked:
            query_pos = q_off + lax.broadcasted_iota(jnp.int32, (sub, q_rows), 1)
            row = lax.broadcasted_iota(jnp.int32, (sub, q_rows), 0)
            visibles = []
            for t in range(head_count):
                key_pos = key_block * KEY_ROWS + ((head - t + head_count) % head_count) * sub + row
                visibles.append((key_pos <= query_pos) & (key_pos >= qstart_ref[...]))
            visibles = [visibles[0], jnp.concatenate(visibles[1:], axis=0)]
        for g in range(groups):
            kcols = slice(g * HEAD_DIM, (g + 1) * HEAD_DIM)
            keys = [k[:, kcols] for k, _ in parts]
            values_t = [v[:, kcols].T for _, v in parts]
            for r in range(heads_per):
                j = g * heads_per + r
                scores = [jnp.dot(k, qt_sc[j], preferred_element_type=jnp.float32) for k in keys]
                if masked:
                    scores = [jnp.where(vis, s, -jnp.inf) for vis, s in zip(visibles, scores)]
                m_old = m_sc[j]
                m_new = jnp.maximum(
                    m_old, jnp.maximum(jnp.max(scores[0], axis=0, keepdims=True), jnp.max(scores[1], axis=0, keepdims=True))
                )
                weights = [jnp.exp2((s - m_new) * scale) for s in scores]
                factor = jnp.exp2((m_old - m_new) * scale)
                l_sc[j] = l_sc[j] * factor + (
                    jnp.sum(weights[0], axis=0, keepdims=True) + jnp.sum(weights[1], axis=0, keepdims=True)
                )
                product = jnp.dot(values_t[0], weights[0].astype(jnp.bfloat16), preferred_element_type=jnp.float32)
                product = product + jnp.dot(
                    values_t[1], weights[1].astype(jnp.bfloat16), preferred_element_type=jnp.float32
                )
                acc_sc[j] = acc_sc[j] * factor + product
                m_sc[j] = m_new

    @pl.when(active & full)
    def _():
        compute(False)

    @pl.when(active & jnp.logical_not(full))
    def _():
        compute(True)

    @pl.when(step == steps - 1)
    def _():
        for j in range(groups * heads_per):
            cols = slice(j * HEAD_DIM, (j + 1) * HEAD_DIM)
            o_ref[:, cols] = (acc_sc[j] / l_sc[j]).T.astype(o_ref.dtype)


def attend(q_tile, q_off, kv_own, kv_rest, doc_ids, groups, heads_per):
    tokens = doc_ids.shape[0]
    q_rows = q_tile.shape[0]
    blocks = tokens // KEY_ROWS
    steps = min(blocks, -(-DOC_MOST // KEY_ROWS) + 1)
    head_count = lax.axis_size("head")
    sub = kv_own.shape[1]
    query_doc = lax.dynamic_slice_in_dim(doc_ids, q_off, q_rows)
    query_start = jnp.sum((doc_ids[None, :] < query_doc[:, None]).astype(jnp.int32), axis=1).reshape(1, q_rows)
    meta = jnp.stack(
        [query_start[0, 0] // KEY_ROWS, (q_off + q_rows - 1) // KEY_ROWS, q_off, lax.axis_index("head")]
    ).astype(jnp.int32)
    width = groups * heads_per * HEAD_DIM
    kv_width = groups * HEAD_DIM
    heads = groups * heads_per
    rest = kv_rest.shape[1]

    def key_index(j, meta, docs):
        return jnp.minimum(meta[0] + j, meta[1])

    kernel = functools.partial(
        flash_kernel, heads_per=heads_per, groups=groups, q_rows=q_rows, steps=steps,
        scale=math.log2(math.e) / HEAD_DIM**0.5, sub=sub, head_count=head_count,
    )
    return pl.pallas_call(
        kernel,
        out_shape=jax.ShapeDtypeStruct((q_rows, width), jnp.bfloat16),
        grid_spec=pltpu.PrefetchScalarGridSpec(
            num_scalar_prefetch=2,
            grid=(steps,),
            in_specs=[
                pl.BlockSpec((q_rows, width), lambda j, meta, docs: (0, 0)),
                pl.BlockSpec((None, sub, kv_width), lambda j, meta, docs: (key_index(j, meta, docs), 0, 0)),
                pl.BlockSpec((None, sub, kv_width), lambda j, meta, docs: (key_index(j, meta, docs), 0, 1)),
                pl.BlockSpec((None, rest, kv_width), lambda j, meta, docs: (key_index(j, meta, docs), 0, 0)),
                pl.BlockSpec((None, rest, kv_width), lambda j, meta, docs: (key_index(j, meta, docs), 0, 1)),
                pl.BlockSpec((1, q_rows), lambda j, meta, docs: (0, 0)),
            ],
            out_specs=pl.BlockSpec((q_rows, width), lambda j, meta, docs: (0, 0)),
            scratch_shapes=[
                pltpu.VMEM((heads, HEAD_DIM, q_rows), jnp.bfloat16),
                pltpu.VMEM((heads, 1, q_rows), jnp.float32),
                pltpu.VMEM((heads, 1, q_rows), jnp.float32),
                pltpu.VMEM((heads, HEAD_DIM, q_rows), jnp.float32),
            ],
        ),
        compiler_params=pltpu.CompilerParams(dimension_semantics=("arbitrary",)),
    )(meta, doc_ids, q_tile, kv_own, kv_own, kv_rest, kv_rest, query_start)


def gather_kv(key_rows, value_rows):
    head_count = lax.axis_size("head")
    head = lax.axis_index("head")
    width = key_rows.shape[1] // head_count
    pieces = []
    for t in range(head_count):
        cols = ((head + t) % head_count) * width
        piece = jnp.concatenate(
            [lax.dynamic_slice_in_dim(key_rows, cols, width, axis=1),
             lax.dynamic_slice_in_dim(value_rows, cols, width, axis=1)], axis=1)
        if t:
            piece = lax.ppermute(piece, "head", [(i, (i + t) % head_count) for i in range(head_count)])
        pieces.append(piece)
    kv_own = lax.all_gather(pieces[0], "seq", axis=0)
    kv_rest = lax.all_gather(jnp.concatenate(pieces[1:], axis=0), "seq", axis=0)
    return kv_own, kv_rest


def body(query_rows, key_rows, value_rows, doc_ids):
    head_count = lax.axis_size("head")
    head = lax.axis_index("head")
    sub = query_rows.shape[0]
    q_width = query_rows.shape[1] // head_count
    groups = key_rows.shape[1] // HEAD_DIM // head_count
    heads_per = query_rows.shape[1] // key_rows.shape[1]
    block_start = lax.axis_index("seq") * sub * head_count
    kv_own, kv_rest = gather_kv(key_rows, value_rows)
    result = jnp.zeros_like(query_rows)
    for t in range(head_count):
        piece = lax.dynamic_slice_in_dim(query_rows, ((head + t) % head_count) * q_width, q_width, axis=1)
        if t:
            piece = lax.ppermute(piece, "head", [(i, (i + t) % head_count) for i in range(head_count)])
        q_off = block_start + ((head - t) % head_count) * sub
        out_tile = attend(piece, q_off, kv_own, kv_rest, doc_ids, groups, heads_per)
        if t:
            out_tile = lax.ppermute(out_tile, "head", [(i, (i - t) % head_count) for i in range(head_count)])
        result = lax.dynamic_update_slice_in_dim(result, out_tile, ((head + t) % head_count) * q_width, axis=1)
    return result


def solution(mesh):
    placed = (P(("seq", "head"), None), P(("seq", "head"), None), P(("seq", "head"), None), P())
    return jax.shard_map(
        body, mesh=mesh, in_specs=placed, out_specs=P(("seq", "head"), None), check_vma=False
    )
```

```python
import functools
import math

import jax
import jax.numpy as jnp
from jax import lax
from jax.experimental import pallas as pl
from jax.experimental.pallas import tpu as pltpu
from jax.sharding import PartitionSpec as P

HEAD_DIM = 128
KEY_ROWS = 512
DOC_MOST = 3584
NEG_START = -1e30


def flash_kernel(meta_ref, doc_ref, qt_ref, k_ref, v_ref, qstart_ref, o_ref, m_sc, l_sc, acc_sc,
                 *, heads_per, groups, q_rows, steps, scale):
    step = pl.program_id(0)
    first_block = meta_ref[0]
    last_block = meta_ref[1]
    q_off = meta_ref[2]
    key_block = jnp.minimum(first_block + step, last_block)
    active = first_block + step <= last_block
    full = (key_block * KEY_ROWS + KEY_ROWS - 1 < q_off) & (
        doc_ref[key_block * KEY_ROWS] == doc_ref[q_off + q_rows - 1]
    )

    @pl.when(step == 0)
    def _():
        m_sc[...] = jnp.full(m_sc.shape, NEG_START, jnp.float32)
        l_sc[...] = jnp.zeros(l_sc.shape, jnp.float32)
        acc_sc[...] = jnp.zeros(acc_sc.shape, jnp.float32)

    def compute(masked):
        if masked:
            key_pos = key_block * KEY_ROWS + lax.broadcasted_iota(jnp.int32, (KEY_ROWS, q_rows), 0)
            query_pos = q_off + lax.broadcasted_iota(jnp.int32, (KEY_ROWS, q_rows), 1)
            visible = (key_pos <= query_pos) & (key_pos >= qstart_ref[...])
        for g in range(groups):
            keys = k_ref[:, g * HEAD_DIM:(g + 1) * HEAD_DIM]
            values_t = v_ref[:, g * HEAD_DIM:(g + 1) * HEAD_DIM].T
            for r in range(heads_per):
                j = g * heads_per + r
                scores = jnp.dot(keys, qt_ref[j], preferred_element_type=jnp.float32)
                if masked:
                    scores = jnp.where(visible, scores, -jnp.inf)
                m_old = m_sc[j]
                m_new = jnp.maximum(m_old, jnp.max(scores, axis=0, keepdims=True))
                weights = jnp.exp2((scores - m_new) * scale)
                factor = jnp.exp2((m_old - m_new) * scale)
                l_sc[j] = l_sc[j] * factor + jnp.sum(weights, axis=0, keepdims=True)
                product = jnp.dot(values_t, weights.astype(jnp.bfloat16), preferred_element_type=jnp.float32)
                acc_sc[j] = acc_sc[j] * factor + product
                m_sc[j] = m_new

    @pl.when(active & full)
    def _():
        compute(False)

    @pl.when(active & jnp.logical_not(full))
    def _():
        compute(True)

    @pl.when(step == steps - 1)
    def _():
        for j in range(groups * heads_per):
            cols = slice(j * HEAD_DIM, (j + 1) * HEAD_DIM)
            o_ref[:, cols] = (acc_sc[j] / l_sc[j]).T.astype(o_ref.dtype)


def attend(q_tile, q_off, kv_rows, doc_ids, groups, heads_per):
    tokens = doc_ids.shape[0]
    q_rows = q_tile.shape[2]
    blocks = tokens // KEY_ROWS
    steps = min(blocks, -(-DOC_MOST // KEY_ROWS) + 1)
    query_doc = lax.dynamic_slice_in_dim(doc_ids, q_off, q_rows)
    query_start = jnp.sum((doc_ids[None, :] < query_doc[:, None]).astype(jnp.int32), axis=1).reshape(1, q_rows)
    meta = jnp.stack([query_start[0, 0] // KEY_ROWS, (q_off + q_rows - 1) // KEY_ROWS, q_off]).astype(jnp.int32)
    width = groups * heads_per * HEAD_DIM
    kv_width = groups * HEAD_DIM
    heads = groups * heads_per

    def key_index(j, meta, docs):
        return jnp.minimum(meta[0] + j, meta[1])

    kernel = functools.partial(
        flash_kernel, heads_per=heads_per, groups=groups, q_rows=q_rows, steps=steps,
        scale=math.log2(math.e) / HEAD_DIM**0.5,
    )
    return pl.pallas_call(
        kernel,
        out_shape=jax.ShapeDtypeStruct((q_rows, width), jnp.bfloat16),
        grid_spec=pltpu.PrefetchScalarGridSpec(
            num_scalar_prefetch=2,
            grid=(steps,),
            in_specs=[
                pl.BlockSpec((groups * heads_per, HEAD_DIM, q_rows), lambda j, meta, docs: (0, 0, 0)),
                pl.BlockSpec((KEY_ROWS, kv_width), lambda j, meta, docs: (key_index(j, meta, docs), 0)),
                pl.BlockSpec((KEY_ROWS, kv_width), lambda j, meta, docs: (key_index(j, meta, docs), 1)),
                pl.BlockSpec((1, q_rows), lambda j, meta, docs: (0, 0)),
            ],
            out_specs=pl.BlockSpec((q_rows, width), lambda j, meta, docs: (0, 0)),
            scratch_shapes=[
                pltpu.VMEM((heads, 1, q_rows), jnp.float32),
                pltpu.VMEM((heads, 1, q_rows), jnp.float32),
                pltpu.VMEM((heads, HEAD_DIM, q_rows), jnp.float32),
            ],
        ),
        compiler_params=pltpu.CompilerParams(dimension_semantics=("arbitrary",)),
    )(meta, doc_ids, q_tile, kv_rows, kv_rows, query_start)


def gather_kv(key_rows, value_rows):
    head_count = lax.axis_size("head")
    head = lax.axis_index("head")
    sub = key_rows.shape[0]
    width = key_rows.shape[1] // head_count
    local = jnp.zeros((head_count * sub, 2 * width), key_rows.dtype)
    for t in range(head_count):
        cols = ((head + t) % head_count) * width
        piece = jnp.concatenate(
            [lax.dynamic_slice_in_dim(key_rows, cols, width, axis=1),
             lax.dynamic_slice_in_dim(value_rows, cols, width, axis=1)], axis=1)
        if t:
            piece = lax.ppermute(piece, "head", [(i, (i + t) % head_count) for i in range(head_count)])
        local = lax.dynamic_update_slice_in_dim(local, piece, ((head - t) % head_count) * sub, axis=0)
    return lax.all_gather(local, "seq", axis=0, tiled=True)


def body(query_rows, key_rows, value_rows, doc_ids):
    head_count = lax.axis_size("head")
    head = lax.axis_index("head")
    sub = query_rows.shape[0]
    q_width = query_rows.shape[1] // head_count
    groups = key_rows.shape[1] // HEAD_DIM // head_count
    heads_per = query_rows.shape[1] // key_rows.shape[1]
    block_start = lax.axis_index("seq") * sub * head_count
    kv_rows = gather_kv(key_rows, value_rows)
    result = jnp.zeros_like(query_rows)
    for t in range(head_count):
        piece = lax.dynamic_slice_in_dim(query_rows, ((head + t) % head_count) * q_width, q_width, axis=1)
        piece = piece.reshape(sub, q_width // HEAD_DIM, HEAD_DIM).transpose(1, 2, 0)
        if t:
            piece = lax.ppermute(piece, "head", [(i, (i + t) % head_count) for i in range(head_count)])
        q_off = block_start + ((head - t) % head_count) * sub
        out_tile = attend(piece, q_off, kv_rows, doc_ids, groups, heads_per)
        if t:
            out_tile = lax.ppermute(out_tile, "head", [(i, (i - t) % head_count) for i in range(head_count)])
        result = lax.dynamic_update_slice_in_dim(result, out_tile, ((head + t) % head_count) * q_width, axis=1)
    return result


def solution(mesh):
    placed = (P(("seq", "head"), None), P(("seq", "head"), None), P(("seq", "head"), None), P())
    return jax.shard_map(
        body, mesh=mesh, in_specs=placed, out_specs=P(("seq", "head"), None), check_vma=False
    )
```

```python
import functools
import math

import jax
import jax.numpy as jnp
from jax import lax
from jax.experimental import pallas as pl
from jax.experimental.pallas import tpu as pltpu
from jax.sharding import PartitionSpec as P

HEAD_DIM = 128
KEY_ROWS = 512
DOC_MOST = 3584
NEG_START = -1e30


def flash_kernel(meta_ref, doc_ref, q_ref, k_ref, v_ref, qstart_ref, o_ref, qt_sc, m_sc, l_sc, acc_sc,
                 *, heads_per, groups, q_rows, steps, scale):
    step = pl.program_id(0)
    first_block = meta_ref[0]
    last_block = meta_ref[1]
    q_off = meta_ref[2]
    key_block = jnp.minimum(first_block + step, last_block)
    active = first_block + step <= last_block
    full = (key_block * KEY_ROWS + KEY_ROWS - 1 < q_off) & (
        doc_ref[key_block * KEY_ROWS] == doc_ref[q_off + q_rows - 1]
    )

    @pl.when(step == 0)
    def _():
        m_sc[...] = jnp.full(m_sc.shape, NEG_START, jnp.float32)
        l_sc[...] = jnp.zeros(l_sc.shape, jnp.float32)
        acc_sc[...] = jnp.zeros(acc_sc.shape, jnp.float32)
        for j in range(groups * heads_per):
            cols = slice(j * HEAD_DIM, (j + 1) * HEAD_DIM)
            qt_sc[j] = q_ref[:, cols].T

    def compute(masked):
        if masked:
            key_pos = key_block * KEY_ROWS + lax.broadcasted_iota(jnp.int32, (KEY_ROWS, q_rows), 0)
            query_pos = q_off + lax.broadcasted_iota(jnp.int32, (KEY_ROWS, q_rows), 1)
            visible = (key_pos <= query_pos) & (key_pos >= qstart_ref[...])
        for g in range(groups):
            keys = k_ref[:, g * HEAD_DIM:(g + 1) * HEAD_DIM]
            values_t = v_ref[:, g * HEAD_DIM:(g + 1) * HEAD_DIM].T
            for r in range(heads_per):
                j = g * heads_per + r
                scores = jnp.dot(keys, qt_sc[j], preferred_element_type=jnp.float32)
                if masked:
                    scores = jnp.where(visible, scores, -jnp.inf)
                m_old = m_sc[j]
                m_new = jnp.maximum(m_old, jnp.max(scores, axis=0, keepdims=True))
                weights = jnp.exp2((scores - m_new) * scale)
                factor = jnp.exp2((m_old - m_new) * scale)
                l_sc[j] = l_sc[j] * factor + jnp.sum(weights, axis=0, keepdims=True)
                product = jnp.dot(values_t, weights.astype(jnp.bfloat16), preferred_element_type=jnp.float32)
                acc_sc[j] = acc_sc[j] * factor + product
                m_sc[j] = m_new

    @pl.when(active & full)
    def _():
        compute(False)

    @pl.when(active & jnp.logical_not(full))
    def _():
        compute(True)

    @pl.when(step == steps - 1)
    def _():
        for j in range(groups * heads_per):
            cols = slice(j * HEAD_DIM, (j + 1) * HEAD_DIM)
            o_ref[:, cols] = (acc_sc[j] / l_sc[j]).T.astype(o_ref.dtype)


def attend(q_tile, q_off, kv_rows, doc_ids, groups, heads_per):
    tokens = doc_ids.shape[0]
    q_rows = q_tile.shape[0]
    blocks = tokens // KEY_ROWS
    steps = min(blocks, -(-DOC_MOST // KEY_ROWS) + 1)
    query_doc = lax.dynamic_slice_in_dim(doc_ids, q_off, q_rows)
    query_start = jnp.sum((doc_ids[None, :] < query_doc[:, None]).astype(jnp.int32), axis=1).reshape(1, q_rows)
    meta = jnp.stack([query_start[0, 0] // KEY_ROWS, (q_off + q_rows - 1) // KEY_ROWS, q_off]).astype(jnp.int32)
    width = groups * heads_per * HEAD_DIM
    kv_width = groups * HEAD_DIM
    heads = groups * heads_per

    def key_index(j, meta, docs):
        return jnp.minimum(meta[0] + j, meta[1])

    kernel = functools.partial(
        flash_kernel, heads_per=heads_per, groups=groups, q_rows=q_rows, steps=steps,
        scale=math.log2(math.e) / HEAD_DIM**0.5,
    )
    return pl.pallas_call(
        kernel,
        out_shape=jax.ShapeDtypeStruct((q_rows, width), jnp.bfloat16),
        grid_spec=pltpu.PrefetchScalarGridSpec(
            num_scalar_prefetch=2,
            grid=(steps,),
            in_specs=[
                pl.BlockSpec((q_rows, width), lambda j, meta, docs: (0, 0)),
                pl.BlockSpec((KEY_ROWS, kv_width), lambda j, meta, docs: (key_index(j, meta, docs), 0)),
                pl.BlockSpec((KEY_ROWS, kv_width), lambda j, meta, docs: (key_index(j, meta, docs), 1)),
                pl.BlockSpec((1, q_rows), lambda j, meta, docs: (0, 0)),
            ],
            out_specs=pl.BlockSpec((q_rows, width), lambda j, meta, docs: (0, 0)),
            scratch_shapes=[
                pltpu.VMEM((heads, HEAD_DIM, q_rows), jnp.bfloat16),
                pltpu.VMEM((heads, 1, q_rows), jnp.float32),
                pltpu.VMEM((heads, 1, q_rows), jnp.float32),
                pltpu.VMEM((heads, HEAD_DIM, q_rows), jnp.float32),
            ],
        ),
        compiler_params=pltpu.CompilerParams(dimension_semantics=("arbitrary",)),
    )(meta, doc_ids, q_tile, kv_rows, kv_rows, query_start)


def gather_kv(key_rows, value_rows):
    head_count = lax.axis_size("head")
    head = lax.axis_index("head")
    sub = key_rows.shape[0]
    width = key_rows.shape[1] // head_count
    local = jnp.zeros((head_count * sub, 2 * width), key_rows.dtype)
    for t in range(head_count):
        cols = ((head + t) % head_count) * width
        piece = jnp.concatenate(
            [lax.dynamic_slice_in_dim(key_rows, cols, width, axis=1),
             lax.dynamic_slice_in_dim(value_rows, cols, width, axis=1)], axis=1)
        if t:
            piece = lax.ppermute(piece, "head", [(i, (i + t) % head_count) for i in range(head_count)])
        local = lax.dynamic_update_slice_in_dim(local, piece, ((head - t) % head_count) * sub, axis=0)
    return lax.all_gather(local, "seq", axis=0, tiled=True)


def body(query_rows, key_rows, value_rows, doc_ids):
    head_count = lax.axis_size("head")
    head = lax.axis_index("head")
    sub = query_rows.shape[0]
    q_width = query_rows.shape[1] // head_count
    groups = key_rows.shape[1] // HEAD_DIM // head_count
    heads_per = query_rows.shape[1] // key_rows.shape[1]
    block_start = lax.axis_index("seq") * sub * head_count
    kv_rows = gather_kv(key_rows, value_rows)
    result = jnp.zeros_like(query_rows)
    for t in range(head_count):
        piece = lax.dynamic_slice_in_dim(query_rows, ((head + t) % head_count) * q_width, q_width, axis=1)
        if t:
            piece = lax.ppermute(piece, "head", [(i, (i + t) % head_count) for i in range(head_count)])
        q_off = block_start + ((head - t) % head_count) * sub
        out_tile = attend(piece, q_off, kv_rows, doc_ids, groups, heads_per)
        if t:
            out_tile = lax.ppermute(out_tile, "head", [(i, (i - t) % head_count) for i in range(head_count)])
        result = lax.dynamic_update_slice_in_dim(result, out_tile, ((head + t) % head_count) * q_width, axis=1)
    return result


def solution(mesh):
    placed = (P(("seq", "head"), None), P(("seq", "head"), None), P(("seq", "head"), None), P())
    return jax.shard_map(
        body, mesh=mesh, in_specs=placed, out_specs=P(("seq", "head"), None), check_vma=False
    )
```

```python
import functools
import math

import jax
import jax.numpy as jnp
from jax import lax
from jax.experimental import pallas as pl
from jax.experimental.pallas import tpu as pltpu
from jax.sharding import PartitionSpec as P

HEAD_DIM = 128
KEY_ROWS = 1024
DOC_MOST = 3584
NEG_START = -1e30


def flash_kernel(meta_ref, doc_ref, q_ref, k_ref, v_ref, qstart_ref, o_ref, qt_sc, m_sc, l_sc, acc_sc,
                 *, heads_per, groups, q_rows, steps, scale):
    step = pl.program_id(0)
    first_block = meta_ref[0]
    last_block = meta_ref[1]
    q_off = meta_ref[2]
    key_block = jnp.minimum(first_block + step, last_block)
    active = first_block + step <= last_block
    full = (key_block * KEY_ROWS + KEY_ROWS - 1 < q_off) & (
        doc_ref[key_block * KEY_ROWS] == doc_ref[q_off + q_rows - 1]
    )

    @pl.when(step == 0)
    def _():
        m_sc[...] = jnp.full(m_sc.shape, NEG_START, jnp.float32)
        l_sc[...] = jnp.zeros(l_sc.shape, jnp.float32)
        acc_sc[...] = jnp.zeros(acc_sc.shape, jnp.float32)
        for j in range(groups * heads_per):
            cols = slice(j * HEAD_DIM, (j + 1) * HEAD_DIM)
            qt_sc[j] = q_ref[:, cols].astype(jnp.float32).T.astype(jnp.bfloat16)

    def compute(masked):
        if masked:
            key_pos = key_block * KEY_ROWS + lax.broadcasted_iota(jnp.int32, (KEY_ROWS, q_rows), 0)
            query_pos = q_off + lax.broadcasted_iota(jnp.int32, (KEY_ROWS, q_rows), 1)
            visible = (key_pos <= query_pos) & (key_pos >= qstart_ref[...])
        for g in range(groups):
            keys = k_ref[:, g * HEAD_DIM:(g + 1) * HEAD_DIM]
            values_t = v_ref[:, g * HEAD_DIM:(g + 1) * HEAD_DIM].T
            for r in range(heads_per):
                j = g * heads_per + r
                scores = jnp.dot(keys, qt_sc[j], preferred_element_type=jnp.float32)
                if masked:
                    scores = jnp.where(visible, scores, -jnp.inf)
                m_old = m_sc[j]
                m_new = jnp.maximum(m_old, jnp.max(scores, axis=0, keepdims=True))
                weights = jnp.exp2((scores - m_new) * scale)
                factor = jnp.exp2((m_old - m_new) * scale)
                l_sc[j] = l_sc[j] * factor + jnp.sum(weights, axis=0, keepdims=True)
                product = jnp.dot(values_t, weights.astype(jnp.bfloat16), preferred_element_type=jnp.float32)
                acc_sc[j] = acc_sc[j] * factor + product
                m_sc[j] = m_new

    @pl.when(active & full)
    def _():
        compute(False)

    @pl.when(active & jnp.logical_not(full))
    def _():
        compute(True)

    @pl.when(step == steps - 1)
    def _():
        for j in range(groups * heads_per):
            cols = slice(j * HEAD_DIM, (j + 1) * HEAD_DIM)
            o_ref[:, cols] = (acc_sc[j] / l_sc[j]).T.astype(o_ref.dtype)


def attend(q_tile, q_off, kv_rows, doc_ids, groups, heads_per):
    tokens = doc_ids.shape[0]
    q_rows = q_tile.shape[0]
    blocks = tokens // KEY_ROWS
    steps = min(blocks, -(-DOC_MOST // KEY_ROWS) + 1)
    query_doc = lax.dynamic_slice_in_dim(doc_ids, q_off, q_rows)
    query_start = jnp.sum((doc_ids[None, :] < query_doc[:, None]).astype(jnp.int32), axis=1).reshape(1, q_rows)
    meta = jnp.stack([query_start[0, 0] // KEY_ROWS, (q_off + q_rows - 1) // KEY_ROWS, q_off]).astype(jnp.int32)
    width = groups * heads_per * HEAD_DIM
    kv_width = groups * HEAD_DIM
    heads = groups * heads_per

    def key_index(j, meta, docs):
        return jnp.minimum(meta[0] + j, meta[1])

    kernel = functools.partial(
        flash_kernel, heads_per=heads_per, groups=groups, q_rows=q_rows, steps=steps,
        scale=math.log2(math.e) / HEAD_DIM**0.5,
    )
    return pl.pallas_call(
        kernel,
        out_shape=jax.ShapeDtypeStruct((q_rows, width), jnp.bfloat16),
        grid_spec=pltpu.PrefetchScalarGridSpec(
            num_scalar_prefetch=2,
            grid=(steps,),
            in_specs=[
                pl.BlockSpec((q_rows, width), lambda j, meta, docs: (0, 0)),
                pl.BlockSpec((KEY_ROWS, kv_width), lambda j, meta, docs: (key_index(j, meta, docs), 0)),
                pl.BlockSpec((KEY_ROWS, kv_width), lambda j, meta, docs: (key_index(j, meta, docs), 1)),
                pl.BlockSpec((1, q_rows), lambda j, meta, docs: (0, 0)),
            ],
            out_specs=pl.BlockSpec((q_rows, width), lambda j, meta, docs: (0, 0)),
            scratch_shapes=[
                pltpu.VMEM((heads, HEAD_DIM, q_rows), jnp.bfloat16),
                pltpu.VMEM((heads, 1, q_rows), jnp.float32),
                pltpu.VMEM((heads, 1, q_rows), jnp.float32),
                pltpu.VMEM((heads, HEAD_DIM, q_rows), jnp.float32),
            ],
        ),
        compiler_params=pltpu.CompilerParams(dimension_semantics=("arbitrary",)),
    )(meta, doc_ids, q_tile, kv_rows, kv_rows, query_start)


def gather_kv(key_rows, value_rows):
    head_count = lax.axis_size("head")
    head = lax.axis_index("head")
    sub = key_rows.shape[0]
    width = key_rows.shape[1] // head_count
    local = jnp.zeros((head_count * sub, 2 * width), key_rows.dtype)
    for t in range(head_count):
        cols = ((head + t) % head_count) * width
        piece = jnp.concatenate(
            [lax.dynamic_slice_in_dim(key_rows, cols, width, axis=1),
             lax.dynamic_slice_in_dim(value_rows, cols, width, axis=1)], axis=1)
        if t:
            piece = lax.ppermute(piece, "head", [(i, (i + t) % head_count) for i in range(head_count)])
        local = lax.dynamic_update_slice_in_dim(local, piece, ((head - t) % head_count) * sub, axis=0)
    return lax.all_gather(local, "seq", axis=0, tiled=True)


def body(query_rows, key_rows, value_rows, doc_ids):
    head_count = lax.axis_size("head")
    head = lax.axis_index("head")
    sub = query_rows.shape[0]
    q_width = query_rows.shape[1] // head_count
    groups = key_rows.shape[1] // HEAD_DIM // head_count
    heads_per = query_rows.shape[1] // key_rows.shape[1]
    block_start = lax.axis_index("seq") * sub * head_count
    kv_rows = gather_kv(key_rows, value_rows)
    result = jnp.zeros_like(query_rows)
    for t in range(head_count):
        piece = lax.dynamic_slice_in_dim(query_rows, ((head + t) % head_count) * q_width, q_width, axis=1)
        if t:
            piece = lax.ppermute(piece, "head", [(i, (i + t) % head_count) for i in range(head_count)])
        q_off = block_start + ((head - t) % head_count) * sub
        out_tile = attend(piece, q_off, kv_rows, doc_ids, groups, heads_per)
        if t:
            out_tile = lax.ppermute(out_tile, "head", [(i, (i - t) % head_count) for i in range(head_count)])
        result = lax.dynamic_update_slice_in_dim(result, out_tile, ((head + t) % head_count) * q_width, axis=1)
    return result


def solution(mesh):
    placed = (P(("seq", "head"), None), P(("seq", "head"), None), P(("seq", "head"), None), P())
    return jax.shard_map(
        body, mesh=mesh, in_specs=placed, out_specs=P(("seq", "head"), None), check_vma=False
    )
```

```python
import functools
import math

import jax
import jax.numpy as jnp
from jax import lax
from jax.experimental import pallas as pl
from jax.experimental.pallas import tpu as pltpu
from jax.sharding import PartitionSpec as P

HEAD_DIM = 128
KEY_ROWS = 512
DOC_MOST = 3584
NEG_START = -1e30


def flash_kernel(meta_ref, doc_ref, q_ref, k_ref, v_ref, qstart_ref, o_ref, qt_sc, m_sc, l_sc, acc_sc,
                 *, heads_per, groups, q_rows, steps, scale):
    step = pl.program_id(0)
    first_block = meta_ref[0]
    last_block = meta_ref[1]
    q_off = meta_ref[2]
    key_block = jnp.minimum(first_block + step, last_block)
    active = first_block + step <= last_block
    full = (key_block * KEY_ROWS + KEY_ROWS - 1 < q_off) & (
        doc_ref[key_block * KEY_ROWS] == doc_ref[q_off + q_rows - 1]
    )

    @pl.when(step == 0)
    def _():
        m_sc[...] = jnp.full(m_sc.shape, NEG_START, jnp.float32)
        l_sc[...] = jnp.zeros(l_sc.shape, jnp.float32)
        acc_sc[...] = jnp.zeros(acc_sc.shape, jnp.float32)
        for j in range(groups * heads_per):
            cols = slice(j * HEAD_DIM, (j + 1) * HEAD_DIM)
            qt_sc[j] = q_ref[:, cols].astype(jnp.float32).T.astype(jnp.bfloat16)

    def compute(masked):
        if masked:
            key_pos = key_block * KEY_ROWS + lax.broadcasted_iota(jnp.int32, (KEY_ROWS, q_rows), 0)
            query_pos = q_off + lax.broadcasted_iota(jnp.int32, (KEY_ROWS, q_rows), 1)
            visible = (key_pos <= query_pos) & (key_pos >= qstart_ref[...])
        for g in range(groups):
            keys = k_ref[:, g * HEAD_DIM:(g + 1) * HEAD_DIM]
            values_t = v_ref[:, g * HEAD_DIM:(g + 1) * HEAD_DIM].T
            for r in range(heads_per):
                j = g * heads_per + r
                scores = jnp.dot(keys, qt_sc[j], preferred_element_type=jnp.float32)
                if masked:
                    scores = jnp.where(visible, scores, -jnp.inf)
                m_old = m_sc[j]
                m_new = jnp.maximum(m_old, jnp.max(scores, axis=0, keepdims=True))
                weights = jnp.exp2((scores - m_new) * scale)
                factor = jnp.exp2((m_old - m_new) * scale)
                l_sc[j] = l_sc[j] * factor + jnp.sum(weights, axis=0, keepdims=True)
                product = jnp.dot(values_t, weights.astype(jnp.bfloat16), preferred_element_type=jnp.float32)
                acc_sc[j] = acc_sc[j] * factor + product
                m_sc[j] = m_new

    @pl.when(active & full)
    def _():
        compute(False)

    @pl.when(active & jnp.logical_not(full))
    def _():
        compute(True)

    @pl.when(step == steps - 1)
    def _():
        for j in range(groups * heads_per):
            cols = slice(j * HEAD_DIM, (j + 1) * HEAD_DIM)
            o_ref[:, cols] = (acc_sc[j] * (1.0 / l_sc[j])).T.astype(o_ref.dtype)


def attend(q_tile, q_off, kv_rows, doc_ids, groups, heads_per):
    tokens = doc_ids.shape[0]
    q_rows = q_tile.shape[0]
    blocks = tokens // KEY_ROWS
    steps = min(blocks, -(-DOC_MOST // KEY_ROWS) + 1)
    query_doc = lax.dynamic_slice_in_dim(doc_ids, q_off, q_rows)
    query_start = jnp.sum((doc_ids[None, :] < query_doc[:, None]).astype(jnp.int32), axis=1).reshape(1, q_rows)
    meta = jnp.stack([query_start[0, 0] // KEY_ROWS, (q_off + q_rows - 1) // KEY_ROWS, q_off]).astype(jnp.int32)
    width = groups * heads_per * HEAD_DIM
    kv_width = groups * HEAD_DIM
    heads = groups * heads_per

    def key_index(j, meta, docs):
        return jnp.minimum(meta[0] + j, meta[1])

    kernel = functools.partial(
        flash_kernel, heads_per=heads_per, groups=groups, q_rows=q_rows, steps=steps,
        scale=math.log2(math.e) / HEAD_DIM**0.5,
    )
    return pl.pallas_call(
        kernel,
        out_shape=jax.ShapeDtypeStruct((q_rows, width), jnp.bfloat16),
        grid_spec=pltpu.PrefetchScalarGridSpec(
            num_scalar_prefetch=2,
            grid=(steps,),
            in_specs=[
                pl.BlockSpec((q_rows, width), lambda j, meta, docs: (0, 0)),
                pl.BlockSpec((KEY_ROWS, kv_width), lambda j, meta, docs: (key_index(j, meta, docs), 0)),
                pl.BlockSpec((KEY_ROWS, kv_width), lambda j, meta, docs: (key_index(j, meta, docs), 1)),
                pl.BlockSpec((1, q_rows), lambda j, meta, docs: (0, 0)),
            ],
            out_specs=pl.BlockSpec((q_rows, width), lambda j, meta, docs: (0, 0)),
            scratch_shapes=[
                pltpu.VMEM((heads, HEAD_DIM, q_rows), jnp.bfloat16),
                pltpu.VMEM((heads, 1, q_rows), jnp.float32),
                pltpu.VMEM((heads, 1, q_rows), jnp.float32),
                pltpu.VMEM((heads, HEAD_DIM, q_rows), jnp.float32),
            ],
        ),
        compiler_params=pltpu.CompilerParams(dimension_semantics=("arbitrary",)),
    )(meta, doc_ids, q_tile, kv_rows, kv_rows, query_start)


def gather_kv(key_rows, value_rows):
    head_count = lax.axis_size("head")
    head = lax.axis_index("head")
    sub = key_rows.shape[0]
    width = key_rows.shape[1] // head_count
    local = jnp.zeros((head_count * sub, 2 * width), key_rows.dtype)
    for t in range(head_count):
        cols = ((head + t) % head_count) * width
        piece = jnp.concatenate(
            [lax.dynamic_slice_in_dim(key_rows, cols, width, axis=1),
             lax.dynamic_slice_in_dim(value_rows, cols, width, axis=1)], axis=1)
        if t:
            piece = lax.ppermute(piece, "head", [(i, (i + t) % head_count) for i in range(head_count)])
        local = lax.dynamic_update_slice_in_dim(local, piece, ((head - t) % head_count) * sub, axis=0)
    return lax.all_gather(local, "seq", axis=0, tiled=True)


def body(query_rows, key_rows, value_rows, doc_ids):
    head_count = lax.axis_size("head")
    head = lax.axis_index("head")
    sub = query_rows.shape[0]
    q_width = query_rows.shape[1] // head_count
    groups = key_rows.shape[1] // HEAD_DIM // head_count
    heads_per = query_rows.shape[1] // key_rows.shape[1]
    block_start = lax.axis_index("seq") * sub * head_count
    kv_rows = gather_kv(key_rows, value_rows)
    result = jnp.zeros_like(query_rows)
    for t in range(head_count):
        piece = lax.dynamic_slice_in_dim(query_rows, ((head + t) % head_count) * q_width, q_width, axis=1)
        if t:
            piece = lax.ppermute(piece, "head", [(i, (i + t) % head_count) for i in range(head_count)])
        q_off = block_start + ((head - t) % head_count) * sub
        out_tile = attend(piece, q_off, kv_rows, doc_ids, groups, heads_per)
        if t:
            out_tile = lax.ppermute(out_tile, "head", [(i, (i - t) % head_count) for i in range(head_count)])
        result = lax.dynamic_update_slice_in_dim(result, out_tile, ((head + t) % head_count) * q_width, axis=1)
    return result


def solution(mesh):
    placed = (P(("seq", "head"), None), P(("seq", "head"), None), P(("seq", "head"), None), P())
    return jax.shard_map(
        body, mesh=mesh, in_specs=placed, out_specs=P(("seq", "head"), None), check_vma=False
    )
```

```python
import functools
import math

import jax
import jax.numpy as jnp
from jax import lax
from jax.experimental import pallas as pl
from jax.experimental.pallas import tpu as pltpu
from jax.sharding import PartitionSpec as P

HEAD_DIM = 128
KEY_ROWS = 512
DOC_MOST = 3584
NEG_START = -1e30


def flash_kernel(meta_ref, doc_ref, q_ref, k_ref, v_ref, qstart_ref, o_ref, qt_sc, m_sc, l_sc, acc_sc,
                 *, heads_per, groups, q_rows, steps, scale):
    step = pl.program_id(0)
    first_block = meta_ref[0]
    last_block = meta_ref[1]
    q_off = meta_ref[2]
    key_block = jnp.minimum(first_block + step, last_block)
    active = first_block + step <= last_block
    full = (key_block * KEY_ROWS + KEY_ROWS - 1 < q_off) & (
        doc_ref[key_block * KEY_ROWS] == doc_ref[q_off + q_rows - 1]
    )

    @pl.when(step == 0)
    def _():
        m_sc[...] = jnp.full(m_sc.shape, NEG_START, jnp.float32)
        l_sc[...] = jnp.zeros(l_sc.shape, jnp.float32)
        acc_sc[...] = jnp.zeros(acc_sc.shape, jnp.float32)
        for j in range(groups * heads_per):
            cols = slice(j * HEAD_DIM, (j + 1) * HEAD_DIM)
            qt_sc[j] = q_ref[:, cols].astype(jnp.float32).T.astype(jnp.bfloat16)

    def compute(masked):
        if masked:
            key_pos = key_block * KEY_ROWS + lax.broadcasted_iota(jnp.int32, (KEY_ROWS, q_rows), 0)
            query_pos = q_off + lax.broadcasted_iota(jnp.int32, (KEY_ROWS, q_rows), 1)
            visible = (key_pos <= query_pos) & (key_pos >= qstart_ref[...])
        for g in range(groups):
            keys = k_ref[:, g * HEAD_DIM:(g + 1) * HEAD_DIM]
            values_t = jnp.concatenate(
                [v_ref[:, g * HEAD_DIM:(g + 1) * HEAD_DIM].T, jnp.ones((8, KEY_ROWS), jnp.bfloat16)], axis=0
            )
            for r in range(heads_per):
                j = g * heads_per + r
                scores = jnp.dot(keys, qt_sc[j], preferred_element_type=jnp.float32)
                if masked:
                    scores = jnp.where(visible, scores, -jnp.inf)
                m_old = m_sc[j]
                m_new = jnp.maximum(m_old, jnp.max(scores, axis=0, keepdims=True))
                weights = jnp.exp2((scores - m_new) * scale)
                factor = jnp.exp2((m_old - m_new) * scale)
                product = jnp.dot(values_t, weights.astype(jnp.bfloat16), preferred_element_type=jnp.float32)
                l_sc[j] = l_sc[j] * factor + product[HEAD_DIM:HEAD_DIM + 1]
                acc_sc[j] = acc_sc[j] * factor + product[:HEAD_DIM]
                m_sc[j] = m_new

    @pl.when(active & full)
    def _():
        compute(False)

    @pl.when(active & jnp.logical_not(full))
    def _():
        compute(True)

    @pl.when(step == steps - 1)
    def _():
        for j in range(groups * heads_per):
            cols = slice(j * HEAD_DIM, (j + 1) * HEAD_DIM)
            o_ref[:, cols] = (acc_sc[j] * (1.0 / l_sc[j])).T.astype(o_ref.dtype)


def attend(q_tile, q_off, kv_rows, doc_ids, groups, heads_per):
    tokens = doc_ids.shape[0]
    q_rows = q_tile.shape[0]
    blocks = tokens // KEY_ROWS
    steps = min(blocks, -(-DOC_MOST // KEY_ROWS) + 1)
    query_doc = lax.dynamic_slice_in_dim(doc_ids, q_off, q_rows)
    query_start = jnp.sum((doc_ids[None, :] < query_doc[:, None]).astype(jnp.int32), axis=1).reshape(1, q_rows)
    meta = jnp.stack([query_start[0, 0] // KEY_ROWS, (q_off + q_rows - 1) // KEY_ROWS, q_off]).astype(jnp.int32)
    width = groups * heads_per * HEAD_DIM
    kv_width = groups * HEAD_DIM
    heads = groups * heads_per

    def key_index(j, meta, docs):
        return jnp.minimum(meta[0] + j, meta[1])

    kernel = functools.partial(
        flash_kernel, heads_per=heads_per, groups=groups, q_rows=q_rows, steps=steps,
        scale=math.log2(math.e) / HEAD_DIM**0.5,
    )
    return pl.pallas_call(
        kernel,
        out_shape=jax.ShapeDtypeStruct((q_rows, width), jnp.bfloat16),
        grid_spec=pltpu.PrefetchScalarGridSpec(
            num_scalar_prefetch=2,
            grid=(steps,),
            in_specs=[
                pl.BlockSpec((q_rows, width), lambda j, meta, docs: (0, 0)),
                pl.BlockSpec((KEY_ROWS, kv_width), lambda j, meta, docs: (key_index(j, meta, docs), 0)),
                pl.BlockSpec((KEY_ROWS, kv_width), lambda j, meta, docs: (key_index(j, meta, docs), 1)),
                pl.BlockSpec((1, q_rows), lambda j, meta, docs: (0, 0)),
            ],
            out_specs=pl.BlockSpec((q_rows, width), lambda j, meta, docs: (0, 0)),
            scratch_shapes=[
                pltpu.VMEM((heads, HEAD_DIM, q_rows), jnp.bfloat16),
                pltpu.VMEM((heads, 1, q_rows), jnp.float32),
                pltpu.VMEM((heads, 1, q_rows), jnp.float32),
                pltpu.VMEM((heads, HEAD_DIM, q_rows), jnp.float32),
            ],
        ),
        compiler_params=pltpu.CompilerParams(dimension_semantics=("arbitrary",)),
    )(meta, doc_ids, q_tile, kv_rows, kv_rows, query_start)


def gather_kv(key_rows, value_rows):
    head_count = lax.axis_size("head")
    head = lax.axis_index("head")
    sub = key_rows.shape[0]
    width = key_rows.shape[1] // head_count
    local = jnp.zeros((head_count * sub, 2 * width), key_rows.dtype)
    for t in range(head_count):
        cols = ((head + t) % head_count) * width
        piece = jnp.concatenate(
            [lax.dynamic_slice_in_dim(key_rows, cols, width, axis=1),
             lax.dynamic_slice_in_dim(value_rows, cols, width, axis=1)], axis=1)
        if t:
            piece = lax.ppermute(piece, "head", [(i, (i + t) % head_count) for i in range(head_count)])
        local = lax.dynamic_update_slice_in_dim(local, piece, ((head - t) % head_count) * sub, axis=0)
    return lax.all_gather(local, "seq", axis=0, tiled=True)


def body(query_rows, key_rows, value_rows, doc_ids):
    head_count = lax.axis_size("head")
    head = lax.axis_index("head")
    sub = query_rows.shape[0]
    q_width = query_rows.shape[1] // head_count
    groups = key_rows.shape[1] // HEAD_DIM // head_count
    heads_per = query_rows.shape[1] // key_rows.shape[1]
    block_start = lax.axis_index("seq") * sub * head_count
    kv_rows = gather_kv(key_rows, value_rows)
    result = jnp.zeros_like(query_rows)
    for t in range(head_count):
        piece = lax.dynamic_slice_in_dim(query_rows, ((head + t) % head_count) * q_width, q_width, axis=1)
        if t:
            piece = lax.ppermute(piece, "head", [(i, (i + t) % head_count) for i in range(head_count)])
        q_off = block_start + ((head - t) % head_count) * sub
        out_tile = attend(piece, q_off, kv_rows, doc_ids, groups, heads_per)
        if t:
            out_tile = lax.ppermute(out_tile, "head", [(i, (i - t) % head_count) for i in range(head_count)])
        result = lax.dynamic_update_slice_in_dim(result, out_tile, ((head + t) % head_count) * q_width, axis=1)
    return result


def solution(mesh):
    placed = (P(("seq", "head"), None), P(("seq", "head"), None), P(("seq", "head"), None), P())
    return jax.shard_map(
        body, mesh=mesh, in_specs=placed, out_specs=P(("seq", "head"), None), check_vma=False
    )
```

```python
import functools
import math

import jax
import jax.numpy as jnp
from jax import lax
from jax.experimental import pallas as pl
from jax.experimental.pallas import tpu as pltpu
from jax.sharding import PartitionSpec as P

HEAD_DIM = 128
KEY_ROWS = 512
DOC_MOST = 3584
NEG_START = -1e30


def flash_kernel(meta_ref, doc_ref, q_ref, k_ref, v_ref, qstart_ref, o_ref, qt_sc, m_sc, l_sc, acc_sc,
                 *, heads_per, groups, q_rows, steps, scale):
    step = pl.program_id(0)
    first_block = meta_ref[0]
    last_block = meta_ref[1]
    q_off = meta_ref[2]
    key_block = jnp.minimum(first_block + step, last_block)
    active = first_block + step <= last_block
    full = (key_block * KEY_ROWS + KEY_ROWS - 1 < q_off) & (
        doc_ref[key_block * KEY_ROWS] == doc_ref[q_off + q_rows - 1]
    )

    @pl.when(step == 0)
    def _():
        m_sc[...] = jnp.full(m_sc.shape, NEG_START, jnp.float32)
        l_sc[...] = jnp.zeros(l_sc.shape, jnp.float32)
        acc_sc[...] = jnp.zeros(acc_sc.shape, jnp.float32)
        for j in range(groups * heads_per):
            cols = slice(j * HEAD_DIM, (j + 1) * HEAD_DIM)
            qt_sc[j] = q_ref[:, cols].astype(jnp.float32).T.astype(jnp.bfloat16)

    def compute(masked):
        if masked:
            key_pos = key_block * KEY_ROWS + lax.broadcasted_iota(jnp.int32, (KEY_ROWS, q_rows), 0)
            query_pos = q_off + lax.broadcasted_iota(jnp.int32, (KEY_ROWS, q_rows), 1)
            visible = (key_pos <= query_pos) & (key_pos >= qstart_ref[...])
        for g in range(groups):
            keys = k_ref[:, g * HEAD_DIM:(g + 1) * HEAD_DIM]
            values_t = v_ref[:, g * HEAD_DIM:(g + 1) * HEAD_DIM].T
            for r in range(heads_per):
                j = g * heads_per + r
                scores = jnp.dot(keys, qt_sc[j], preferred_element_type=jnp.float32)
                if masked:
                    scores = jnp.where(visible, scores, -jnp.inf)
                m_old = m_sc[j]
                m_new = jnp.maximum(m_old, jnp.max(scores, axis=0, keepdims=True))
                weights = jnp.exp2((scores - m_new) * scale)
                factor = jnp.exp2((m_old - m_new) * scale)
                l_sc[j] = l_sc[j] * factor + jnp.sum(weights, axis=0, keepdims=True)
                product = jnp.dot(values_t, weights.astype(jnp.bfloat16), preferred_element_type=jnp.float32)
                acc_sc[j] = acc_sc[j] * factor + product
                m_sc[j] = m_new

    @pl.when(active & full)
    def _():
        compute(False)

    @pl.when(active & jnp.logical_not(full))
    def _():
        compute(True)

    @pl.when(step == steps - 1)
    def _():
        for j in range(groups * heads_per):
            cols = slice(j * HEAD_DIM, (j + 1) * HEAD_DIM)
            o_ref[:, cols] = (acc_sc[j] * (1.0 / l_sc[j])).astype(o_ref.dtype).T


def attend(q_tile, q_off, kv_rows, doc_ids, groups, heads_per):
    tokens = doc_ids.shape[0]
    q_rows = q_tile.shape[0]
    blocks = tokens // KEY_ROWS
    steps = min(blocks, -(-DOC_MOST // KEY_ROWS) + 1)
    query_doc = lax.dynamic_slice_in_dim(doc_ids, q_off, q_rows)
    query_start = jnp.sum((doc_ids[None, :] < query_doc[:, None]).astype(jnp.int32), axis=1).reshape(1, q_rows)
    meta = jnp.stack([query_start[0, 0] // KEY_ROWS, (q_off + q_rows - 1) // KEY_ROWS, q_off]).astype(jnp.int32)
    width = groups * heads_per * HEAD_DIM
    kv_width = groups * HEAD_DIM
    heads = groups * heads_per

    def key_index(j, meta, docs):
        return jnp.minimum(meta[0] + j, meta[1])

    kernel = functools.partial(
        flash_kernel, heads_per=heads_per, groups=groups, q_rows=q_rows, steps=steps,
        scale=math.log2(math.e) / HEAD_DIM**0.5,
    )
    return pl.pallas_call(
        kernel,
        out_shape=jax.ShapeDtypeStruct((q_rows, width), jnp.bfloat16),
        grid_spec=pltpu.PrefetchScalarGridSpec(
            num_scalar_prefetch=2,
            grid=(steps,),
            in_specs=[
                pl.BlockSpec((q_rows, width), lambda j, meta, docs: (0, 0)),
                pl.BlockSpec((KEY_ROWS, kv_width), lambda j, meta, docs: (key_index(j, meta, docs), 0)),
                pl.BlockSpec((KEY_ROWS, kv_width), lambda j, meta, docs: (key_index(j, meta, docs), 1)),
                pl.BlockSpec((1, q_rows), lambda j, meta, docs: (0, 0)),
            ],
            out_specs=pl.BlockSpec((q_rows, width), lambda j, meta, docs: (0, 0)),
            scratch_shapes=[
                pltpu.VMEM((heads, HEAD_DIM, q_rows), jnp.bfloat16),
                pltpu.VMEM((heads, 1, q_rows), jnp.float32),
                pltpu.VMEM((heads, 1, q_rows), jnp.float32),
                pltpu.VMEM((heads, HEAD_DIM, q_rows), jnp.float32),
            ],
        ),
        compiler_params=pltpu.CompilerParams(dimension_semantics=("arbitrary",)),
    )(meta, doc_ids, q_tile, kv_rows, kv_rows, query_start)


def gather_kv(key_rows, value_rows):
    head_count = lax.axis_size("head")
    head = lax.axis_index("head")
    sub = key_rows.shape[0]
    width = key_rows.shape[1] // head_count
    local = jnp.zeros((head_count * sub, 2 * width), key_rows.dtype)
    for t in range(head_count):
        cols = ((head + t) % head_count) * width
        piece = jnp.concatenate(
            [lax.dynamic_slice_in_dim(key_rows, cols, width, axis=1),
             lax.dynamic_slice_in_dim(value_rows, cols, width, axis=1)], axis=1)
        if t:
            piece = lax.ppermute(piece, "head", [(i, (i + t) % head_count) for i in range(head_count)])
        local = lax.dynamic_update_slice_in_dim(local, piece, ((head - t) % head_count) * sub, axis=0)
    return lax.all_gather(local, "seq", axis=0, tiled=True)


def body(query_rows, key_rows, value_rows, doc_ids):
    head_count = lax.axis_size("head")
    head = lax.axis_index("head")
    sub = query_rows.shape[0]
    q_width = query_rows.shape[1] // head_count
    groups = key_rows.shape[1] // HEAD_DIM // head_count
    heads_per = query_rows.shape[1] // key_rows.shape[1]
    block_start = lax.axis_index("seq") * sub * head_count
    kv_rows = gather_kv(key_rows, value_rows)
    result = jnp.zeros_like(query_rows)
    for t in range(head_count):
        piece = lax.dynamic_slice_in_dim(query_rows, ((head + t) % head_count) * q_width, q_width, axis=1)
        if t:
            piece = lax.ppermute(piece, "head", [(i, (i + t) % head_count) for i in range(head_count)])
        q_off = block_start + ((head - t) % head_count) * sub
        out_tile = attend(piece, q_off, kv_rows, doc_ids, groups, heads_per)
        if t:
            out_tile = lax.ppermute(out_tile, "head", [(i, (i - t) % head_count) for i in range(head_count)])
        result = lax.dynamic_update_slice_in_dim(result, out_tile, ((head + t) % head_count) * q_width, axis=1)
    return result


def solution(mesh):
    placed = (P(("seq", "head"), None), P(("seq", "head"), None), P(("seq", "head"), None), P())
    return jax.shard_map(
        body, mesh=mesh, in_specs=placed, out_specs=P(("seq", "head"), None), check_vma=False
    )
```
